512 devices in a mesh: segment: 2 (over core), inline: 64 (over x, z), xline: 4 (over y).
Axes of the slice: x: 4, y: 4, z: 16, core: 2. Of those that a mesh axis runs over, the one named last changes fastest.
Arguments:
- survey: float32 [2, 256, 16, 1024], P(None, 'inline', 'xline'), may hold values from -6 to 6
- conduct: bfloat16 [3, 2, 256, 16, 1024], P(None, None, 'inline', 'xline'), may hold values from 0.099609375 to 1
- widths: int32 [2, 64], P(None, 'inline'), may hold values from 2 to 4, as said below
Outputs:
- coherence: float32 [2, 256, 16, 1024], P('segment', 'inline', 'xline')
- curvature: float32 [2, 256, 16, 1024], P('segment', 'inline', 'xline')
The draws below stay inside these ranges and needn't reach their ends.
Inputs may be any that keep to these rules, and one draw needn't show every extreme that they name: `widths`: in every micro-batch some device holds exactly 4 live rows and another exactly 2.
All inputs are finite; a program needn't handle non-finite values.
Results may differ from the reference program's by a relative error of at most 0.0003.
Values sent between devices are 32-bit elements; how exact they have to be, the bound alone decides.
No kernel may reach another device: no remote copies, remote signals or barrier semaphores. Data moves between devices by JAX's collectives and lax.ppermute only.
A program may use at most 64 MiB of HBM per device.

```python
import math
import jax
import jax.numpy as jnp

SLAB = 4
NT = 1024
STEPS = 2
MB = 2
NI = 256
NX = 16
N_INLINE = 64


def draw_widths(key, part):
    first_key, second_key = jax.random.split(jax.random.fold_in(key, 11))
    values = jax.random.randint(first_key, (MB, N_INLINE), SLAB // 2, SLAB + 1)
    spot = jax.random.randint(second_key, (MB,), 0, N_INLINE)
    columns = jnp.arange(N_INLINE)[None, :]
    values = jnp.where(columns == spot[:, None], SLAB, values)
    values = jnp.where(columns == ((spot + 1) % N_INLINE)[:, None], SLAB // 2, values)
    return values.astype(jnp.int32)


def level_of(rng, extent, cuts, smallest, top_value):
    def one(axis_at, shards_of):
        heights = jax.random.uniform(jax.random.fold_in(jax.random.fold_in(rng, 6), axis_at), (shards_of,), jnp.float32, smallest / len(cuts), top_value / len(cuts))
        return jnp.repeat(jnp.exp(heights), extent[axis_at] // shards_of).reshape((-1,) + (1,) * (len(extent) - axis_at - 1))

    gain = one(*cuts[0])
    for cut in cuts[1:]:
        gain = gain * one(*cut)
    return gain


def centred(rng, shape, spread, limit, shards=(), kind=jnp.bfloat16):
    level = level_of(rng, shape, shards, -0.22, 0.18) if shards else 1.0
    values = jax.random.normal(rng, shape, jnp.float32) * spread * level
    return jnp.minimum(jnp.maximum(values, -limit), limit).astype(kind)


def setup_inputs(seed: int = 0) -> dict:
    streams_of = jax.random.split(jax.random.key(seed), 4)
    survey = centred(streams_of[0], (MB, NI, NX, NT), 1.0, 6.0, ((1, 64), (2, 4)), jnp.float32)
    conduct = jnp.clip(jnp.exp(math.log(1.0) - 2.306499 * jax.random.uniform(streams_of[1], (3, MB, NI, NX, NT), jnp.float32) ** level_of(streams_of[1], (3, MB, NI, NX, NT), ((2, 64), (3, 4)), -0.2, 0.2)), 0.099609375, 1.0).astype(jnp.bfloat16)
    widths = draw_widths(jax.random.fold_in(streams_of[3], 71), 0)
    return dict(survey=survey, conduct=conduct, widths=widths)


step_size = 0.15
epsilon = 1e-6


def links(width_row):
    rows_all = SLAB * N_INLINE
    cell = jnp.arange(rows_all, dtype=jnp.int32)
    device = cell // SLAB
    within = cell % SLAB
    width = width_row[device]
    later = jnp.where(within < width - 1, cell + 1, jnp.where(device < N_INLINE - 1, (device + 1) * SLAB, cell)).astype(jnp.int32)
    before_width = width_row[jnp.maximum(device - 1, 0)]
    earlier = jnp.where(within > 0, cell - 1, jnp.where(device > 0, (device - 1) * SLAB + before_width - 1, cell)).astype(jnp.int32)
    return later, earlier, within < width


def clamped(length):
    index = jnp.arange(length, dtype=jnp.int32)
    return jnp.minimum(index + 1, length - 1).astype(jnp.int32), jnp.maximum(index - 1, 0).astype(jnp.int32)


def single_batch(field, coeffs, width_row):
    later, earlier, live = links(width_row)
    pairs = [(later, earlier), clamped(NX), clamped(NT)]
    live_cells = live[:, None, None]
    values = jnp.where(live_cells, field, 0.0)
    for repeat in range(STEPS):
        change = jnp.zeros_like(values)
        for which_axis in range(3):
            kk = coeffs[which_axis]
            for index in pairs[which_axis]:
                change = change + 0.5 * (kk + jnp.take(kk, index, axis=which_axis)) * (jnp.take(values, index, axis=which_axis) - values)
        values = values + step_size * change
    smooth = values
    grads = []
    for which_axis in range(3):
        up_index, down_index = pairs[which_axis]
        grads.append(0.5 * (jnp.take(smooth, up_index, axis=which_axis) - jnp.take(smooth, down_index, axis=which_axis)))
    seconds = []
    for which_axis in range(2):
        up_index, down_index = pairs[which_axis]
        seconds.append(jnp.take(smooth, up_index, axis=which_axis) + jnp.take(smooth, down_index, axis=which_axis) - 2.0 * smooth)
    combos = [(0, 0), (1, 1), (2, 2), (0, 1), (0, 2), (1, 2)]
    tensor = []
    for first_index, second_index in combos:
        member = grads[first_index] * grads[second_index]
        for which_axis in range(3):
            up_index, down_index = pairs[which_axis]
            member = 0.25 * (jnp.take(member, up_index, axis=which_axis) + 2.0 * member + jnp.take(member, down_index, axis=which_axis))
        tensor.append(member)
    trace = tensor[0] + tensor[1] + tensor[2]
    minors = tensor[0] * tensor[1] - tensor[3] * tensor[3] + tensor[0] * tensor[2] - tensor[4] * tensor[4] + tensor[1] * tensor[2] - tensor[5] * tensor[5]
    coherence = 1.0 - 3.0 * minors / (trace * trace + epsilon)
    curvature = (seconds[0] + seconds[1]) / (1.0 + grads[0] * grads[0] + grads[1] * grads[1]) ** 1.5
    return jnp.where(live_cells, coherence, 0.0), jnp.where(live_cells, curvature, 0.0)


def reference(survey, conduct, widths):
    coherent_list = []
    curved_list = []
    for batch in range(MB):
        coeffs = conduct[:, batch].astype(jnp.float32)
        coherence, curvature = single_batch(survey[batch], coeffs, widths[batch])
        coherent_list.append(coherence)
        curved_list.append(curvature)
    return jnp.stack(coherent_list, 0), jnp.stack(curved_list, 0)
```

```python
import jax
import jax.numpy as jnp
from jax import lax
from jax.sharding import PartitionSpec as P

STEPS = 2
HALO = 2


step_size = 0.15
epsilon = 1e-06


def shifted(source, which_axis, offset):
    length = source.shape[which_axis]
    margins = [(0, 0)] * source.ndim
    if offset > 0:
        margins[which_axis] = (0, offset)
        padded = jnp.pad(source, margins)
        return lax.slice_in_dim(padded, offset, offset + length, axis=which_axis)
    margins[which_axis] = (-offset, 0)
    padded = jnp.pad(source, margins)
    return lax.slice_in_dim(padded, 0, length, axis=which_axis)


def neighbor(source, which_axis, offset, opened):
    return jnp.where(opened, shifted(source, which_axis, offset), source)


def moved(value, d_inline, d_xline):
    n_i = lax.axis_size("inline")
    n_x = lax.axis_size("xline")
    if d_xline == 0:
        pairs = [(i, i + d_inline) for i in range(n_i) if 0 <= i + d_inline < n_i]
        return lax.ppermute(value, "inline", pairs)
    if d_inline == 0:
        pairs = [(x, x + d_xline) for x in range(n_x) if 0 <= x + d_xline < n_x]
        return lax.ppermute(value, "xline", pairs)
    pairs = []
    for i in range(n_i):
        for x in range(n_x):
            ti, tx = i + d_inline, x + d_xline
            if 0 <= ti < n_i and 0 <= tx < n_x:
                pairs.append((i * n_x + x, ti * n_x + tx))
    return lax.ppermute(value, ("inline", "xline"), pairs)


def gathered(block, width, corner):
    h = HALO
    rows, cols = block.shape[-3], block.shape[-2]
    ra, ca = block.ndim - 3, block.ndim - 2
    lead = block.shape[:-3]
    samples = block.shape[-1]
    last_rows = lax.dynamic_slice_in_dim(block, width - h, h, ra)
    first_rows = lax.slice_in_dim(block, 0, h, axis=ra)

    def cols_of(value, start, count):
        return lax.slice_in_dim(value, start, start + count, axis=ca)

    def corner_piece(rows_part, from_high_cols):
        start = cols - corner if from_high_cols else 0
        return cols_of(rows_part, start, corner)

    from_prev = moved(last_rows, 1, 0)
    from_next = moved(first_rows, -1, 0)
    from_left = moved(cols_of(block, cols - h, h), 0, 1)
    from_right = moved(cols_of(block, 0, h), 0, -1)
    c_prev_left = moved(corner_piece(lax.slice_in_dim(last_rows, h - corner, h, axis=ra), True), 1, 1)
    c_prev_right = moved(corner_piece(lax.slice_in_dim(last_rows, h - corner, h, axis=ra), False), 1, -1)
    c_next_left = moved(corner_piece(lax.slice_in_dim(first_rows, 0, corner, axis=ra), True), -1, 1)
    c_next_right = moved(corner_piece(lax.slice_in_dim(first_rows, 0, corner, axis=ra), False), -1, -1)

    def zeros(r, c):
        return jnp.zeros(lead + (r, c, samples), block.dtype)

    def band(top, middle, bottom):
        stacked = jnp.concatenate([top, middle, zeros(h, middle.shape[ca])], ra)
        return lax.dynamic_update_slice_in_dim(stacked, bottom, h + width, ra)

    def pad_corner(piece, at_high_cols, at_high_rows):
        row_pad = (0, h - corner) if at_high_rows else (h - corner, 0)
        col_pad = (0, h - corner) if at_high_cols else (h - corner, 0)
        margins = [(0, 0)] * len(lead) + [row_pad, col_pad, (0, 0)]
        return jnp.pad(piece, margins)

    center = band(from_prev, block, from_next)
    left = band(pad_corner(c_prev_left, False, False), from_left, pad_corner(c_next_left, False, True))
    right = band(pad_corner(c_prev_right, True, False), from_right, pad_corner(c_next_right, True, True))
    return jnp.concatenate([left, center, right], ca)


def face_masks(width, rows, cols, samples):
    h = HALO
    inline_pos = lax.axis_index("inline")
    inline_count = lax.axis_size("inline")
    xline_pos = lax.axis_index("xline")
    xline_count = lax.axis_size("xline")
    own_row = jnp.arange(rows + 2 * h, dtype=jnp.int32) - h
    row_up = jnp.logical_not((inline_pos == inline_count - 1) & (own_row == width - 1))
    row_down = jnp.logical_not((inline_pos == 0) & (own_row == 0))
    own_col = jnp.arange(cols + 2 * h, dtype=jnp.int32) - h
    col_up = jnp.logical_not((xline_pos == xline_count - 1) & (own_col == cols - 1))
    col_down = jnp.logical_not((xline_pos == 0) & (own_col == 0))
    sample = jnp.arange(samples, dtype=jnp.int32)
    return [
        (row_up[:, None, None], row_down[:, None, None]),
        (col_up[None, :, None], col_down[None, :, None]),
        ((sample < samples - 1)[None, None, :], (sample > 0)[None, None, :]),
    ]


def relax_step(values, coeffs, masks):
    change = jnp.zeros_like(values)
    for which_axis in range(3):
        kk = coeffs[which_axis]
        up_open, down_open = masks[which_axis]
        for offset, opened in ((1, up_open), (-1, down_open)):
            change = change + 0.5 * (kk + neighbor(kk, which_axis, offset, opened)) * (
                neighbor(values, which_axis, offset, opened) - values
            )
    return values + step_size * change


def attributes(grown, masks):
    grads = []
    for which_axis in range(3):
        up_open, down_open = masks[which_axis]
        grads.append(
            0.5
            * (neighbor(grown, which_axis, 1, up_open) - neighbor(grown, which_axis, -1, down_open))
        )
    seconds = []
    for which_axis in range(2):
        up_open, down_open = masks[which_axis]
        seconds.append(
            neighbor(grown, which_axis, 1, up_open)
            + neighbor(grown, which_axis, -1, down_open)
            - 2.0 * grown
        )
    combos = [(0, 0), (1, 1), (2, 2), (0, 1), (0, 2), (1, 2)]
    tensor = jnp.stack(
        [grads[first_index] * grads[second_index] for first_index, second_index in combos], 0
    )
    for which_axis in range(3):
        up_open, down_open = masks[which_axis]
        tensor = 0.25 * (
            neighbor(tensor, which_axis + 1, 1, up_open)
            + 2.0 * tensor
            + neighbor(tensor, which_axis + 1, -1, down_open)
        )
    trace = tensor[0] + tensor[1] + tensor[2]
    minors = (
        tensor[0] * tensor[1]
        - tensor[3] * tensor[3]
        + tensor[0] * tensor[2]
        - tensor[4] * tensor[4]
        + tensor[1] * tensor[2]
        - tensor[5] * tensor[5]
    )
    coherence = 1.0 - 3.0 * minors / (trace * trace + epsilon)
    curvature = (seconds[0] + seconds[1]) / (1.0 + grads[0] * grads[0] + grads[1] * grads[1]) ** 1.5
    return coherence, curvature


def on_device(survey, conduct, widths):
    h = HALO
    batch = lax.axis_index("segment")
    field = lax.dynamic_index_in_dim(survey, batch, 0, keepdims=False)
    coeffs = lax.dynamic_index_in_dim(conduct, batch, 1, keepdims=False).astype(jnp.float32)
    width = lax.dynamic_index_in_dim(widths[:, 0], batch, 0, keepdims=False)
    rows, cols, samples = field.shape
    live = (jnp.arange(rows, dtype=jnp.int32) < width)[:, None, None]
    masks = face_masks(width, rows, cols, samples)

    values = jnp.where(live, field, 0.0)
    grown = gathered(jnp.concatenate([values[None], coeffs], 0), width, 1)
    values, coeffs_grown = grown[0], grown[1:]
    for repeat in range(STEPS):
        values = relax_step(values, coeffs_grown, masks)
    smooth = values[h : h + rows, h : h + cols]

    grown = gathered(smooth, width, h)
    coherence, curvature = attributes(grown, masks)
    outcome = jnp.stack([coherence, curvature], 0)[:, h : h + rows, h : h + cols]
    outcome = jnp.where(live[None], outcome, 0.0)
    return (outcome[0][None], outcome[1][None])


def solution(mesh):
    placed = (
        P(None, "inline", "xline", None),
        P(None, None, "inline", "xline", None),
        P(None, "inline"),
    )
    return jax.shard_map(
        on_device,
        mesh=mesh,
        in_specs=placed,
        out_specs=(P("segment", "inline", "xline", None), P("segment", "inline", "xline", None)),
        check_vma=False,
    )
```

```python
import jax
import jax.numpy as jnp
from jax import lax
from jax.sharding import PartitionSpec as P

STEPS = 2
HALO = 2


step_size = 0.15
epsilon = 1e-06


def shifted(source, which_axis, offset):
    length = source.shape[which_axis]
    margins = [(0, 0)] * source.ndim
    if offset > 0:
        margins[which_axis] = (0, offset)
        padded = jnp.pad(source, margins)
        return lax.slice_in_dim(padded, offset, offset + length, axis=which_axis)
    margins[which_axis] = (-offset, 0)
    padded = jnp.pad(source, margins)
    return lax.slice_in_dim(padded, 0, length, axis=which_axis)


def neighbor(source, which_axis, offset, opened):
    return jnp.where(opened, shifted(source, which_axis, offset), source)


def moved(value, d_inline, d_xline):
    n_i = lax.axis_size("inline")
    n_x = lax.axis_size("xline")
    if d_xline == 0:
        pairs = [(i, i + d_inline) for i in range(n_i) if 0 <= i + d_inline < n_i]
        return lax.ppermute(value, "inline", pairs)
    if d_inline == 0:
        pairs = [(x, x + d_xline) for x in range(n_x) if 0 <= x + d_xline < n_x]
        return lax.ppermute(value, "xline", pairs)
    pairs = []
    for i in range(n_i):
        for x in range(n_x):
            ti, tx = i + d_inline, x + d_xline
            if 0 <= ti < n_i and 0 <= tx < n_x:
                pairs.append((i * n_x + x, ti * n_x + tx))
    return lax.ppermute(value, ("inline", "xline"), pairs)


def gathered(block, width):
    h = HALO
    rows, cols = block.shape[-3], block.shape[-2]
    ra, ca = block.ndim - 3, block.ndim - 2
    from_left = moved(lax.slice_in_dim(block, cols - h, cols, axis=ca), 0, 1)
    from_right = moved(lax.slice_in_dim(block, 0, h, axis=ca), 0, -1)
    wide = jnp.concatenate([from_left, block, from_right], ca)
    from_prev = moved(lax.dynamic_slice_in_dim(wide, width - h, h, ra), 1, 0)
    from_next = moved(lax.slice_in_dim(wide, 0, h, axis=ra), -1, 0)
    tail = jnp.zeros_like(from_next)
    stacked = jnp.concatenate([from_prev, wide, tail], ra)
    return lax.dynamic_update_slice_in_dim(stacked, from_next, h + width, ra)


def face_masks(width, rows, cols, samples):
    h = HALO
    inline_pos = lax.axis_index("inline")
    inline_count = lax.axis_size("inline")
    xline_pos = lax.axis_index("xline")
    xline_count = lax.axis_size("xline")
    own_row = jnp.arange(rows + 2 * h, dtype=jnp.int32) - h
    row_up = jnp.logical_not((inline_pos == inline_count - 1) & (own_row == width - 1))
    row_down = jnp.logical_not((inline_pos == 0) & (own_row == 0))
    own_col = jnp.arange(cols + 2 * h, dtype=jnp.int32) - h
    col_up = jnp.logical_not((xline_pos == xline_count - 1) & (own_col == cols - 1))
    col_down = jnp.logical_not((xline_pos == 0) & (own_col == 0))
    sample = jnp.arange(samples, dtype=jnp.int32)
    return [
        (row_up[:, None, None], row_down[:, None, None]),
        (col_up[None, :, None], col_down[None, :, None]),
        ((sample < samples - 1)[None, None, :], (sample > 0)[None, None, :]),
    ]


def relax_step(values, coeffs, masks):
    change = jnp.zeros_like(values)
    for which_axis in range(3):
        kk = coeffs[which_axis]
        up_open, down_open = masks[which_axis]
        for offset, opened in ((1, up_open), (-1, down_open)):
            change = change + 0.5 * (kk + neighbor(kk, which_axis, offset, opened)) * (
                neighbor(values, which_axis, offset, opened) - values
            )
    return values + step_size * change


def attributes(grown, masks):
    grads = []
    for which_axis in range(3):
        up_open, down_open = masks[which_axis]
        grads.append(
            0.5
            * (neighbor(grown, which_axis, 1, up_open) - neighbor(grown, which_axis, -1, down_open))
        )
    seconds = []
    for which_axis in range(2):
        up_open, down_open = masks[which_axis]
        seconds.append(
            neighbor(grown, which_axis, 1, up_open)
            + neighbor(grown, which_axis, -1, down_open)
            - 2.0 * grown
        )
    combos = [(0, 0), (1, 1), (2, 2), (0, 1), (0, 2), (1, 2)]
    tensor = jnp.stack(
        [grads[first_index] * grads[second_index] for first_index, second_index in combos], 0
    )
    for which_axis in range(3):
        up_open, down_open = masks[which_axis]
        tensor = 0.25 * (
            neighbor(tensor, which_axis + 1, 1, up_open)
            + 2.0 * tensor
            + neighbor(tensor, which_axis + 1, -1, down_open)
        )
    trace = tensor[0] + tensor[1] + tensor[2]
    minors = (
        tensor[0] * tensor[1]
        - tensor[3] * tensor[3]
        + tensor[0] * tensor[2]
        - tensor[4] * tensor[4]
        + tensor[1] * tensor[2]
        - tensor[5] * tensor[5]
    )
    coherence = 1.0 - 3.0 * minors / (trace * trace + epsilon)
    curvature = (seconds[0] + seconds[1]) / (1.0 + grads[0] * grads[0] + grads[1] * grads[1]) ** 1.5
    return coherence, curvature


def on_device(survey, conduct, widths):
    h = HALO
    batch = lax.axis_index("segment")
    field = lax.dynamic_index_in_dim(survey, batch, 0, keepdims=False)
    coeffs = lax.dynamic_index_in_dim(conduct, batch, 1, keepdims=False).astype(jnp.float32)
    width = lax.dynamic_index_in_dim(widths[:, 0], batch, 0, keepdims=False)
    rows, cols, samples = field.shape
    live = (jnp.arange(rows, dtype=jnp.int32) < width)[:, None, None]
    masks = face_masks(width, rows, cols, samples)

    values = jnp.where(live, field, 0.0)
    grown = gathered(jnp.concatenate([values[None], coeffs], 0), width)
    values, coeffs_grown = grown[0], grown[1:]
    for repeat in range(STEPS):
        values = relax_step(values, coeffs_grown, masks)
    smooth = values[h : h + rows, h : h + cols]

    grown = gathered(smooth, width)
    coherence, curvature = attributes(grown, masks)
    outcome = jnp.stack([coherence, curvature], 0)[:, h : h + rows, h : h + cols]
    outcome = jnp.where(live[None], outcome, 0.0)
    return (outcome[0][None], outcome[1][None])


def solution(mesh):
    placed = (
        P(None, "inline", "xline", None),
        P(None, None, "inline", "xline", None),
        P(None, "inline"),
    )
    return jax.shard_map(
        on_device,
        mesh=mesh,
        in_specs=placed,
        out_specs=(P("segment", "inline", "xline", None), P("segment", "inline", "xline", None)),
        check_vma=False,
    )
```

```python
import jax
import jax.numpy as jnp
from jax import lax
from jax.sharding import PartitionSpec as P

STEPS = 2
HALO = 2


step_size = 0.15
epsilon = 1e-06


def shifted(source, which_axis, offset):
    length = source.shape[which_axis]
    margins = [(0, 0)] * source.ndim
    if offset > 0:
        margins[which_axis] = (0, offset)
        padded = jnp.pad(source, margins)
        return lax.slice_in_dim(padded, offset, offset + length, axis=which_axis)
    margins[which_axis] = (-offset, 0)
    padded = jnp.pad(source, margins)
    return lax.slice_in_dim(padded, 0, length, axis=which_axis)


def neighbor(source, which_axis, offset, opened):
    return jnp.where(opened, shifted(source, which_axis, offset), source)


def moved(value, d_inline, d_xline):
    n_i = lax.axis_size("inline")
    n_x = lax.axis_size("xline")
    if d_xline == 0:
        pairs = [(i, i + d_inline) for i in range(n_i) if 0 <= i + d_inline < n_i]
        return lax.ppermute(value, "inline", pairs)
    if d_inline == 0:
        pairs = [(x, x + d_xline) for x in range(n_x) if 0 <= x + d_xline < n_x]
        return lax.ppermute(value, "xline", pairs)
    pairs = []
    for i in range(n_i):
        for x in range(n_x):
            ti, tx = i + d_inline, x + d_xline
            if 0 <= ti < n_i and 0 <= tx < n_x:
                pairs.append((i * n_x + x, ti * n_x + tx))
    return lax.ppermute(value, ("inline", "xline"), pairs)


def with_columns(block, depth):
    ca = block.ndim - 2
    cols = block.shape[ca]
    from_left = moved(lax.slice_in_dim(block, cols - depth, cols, axis=ca), 0, 1)
    from_right = moved(lax.slice_in_dim(block, 0, depth, axis=ca), 0, -1)
    return jnp.concatenate([from_left, block, from_right], ca)


def with_rows(block, width, depth):
    ra = block.ndim - 3
    from_prev = moved(lax.dynamic_slice_in_dim(block, width - depth, depth, ra), 1, 0)
    from_next = moved(lax.slice_in_dim(block, 0, depth, axis=ra), -1, 0)
    stacked = jnp.concatenate([from_prev, block, jnp.zeros_like(from_next)], ra)
    return lax.dynamic_update_slice_in_dim(stacked, from_next, depth + width, ra)


def face_masks(width, rows, cols, samples, row_halo, col_halo):
    inline_pos = lax.axis_index("inline")
    inline_count = lax.axis_size("inline")
    xline_pos = lax.axis_index("xline")
    xline_count = lax.axis_size("xline")
    own_row = jnp.arange(rows + 2 * row_halo, dtype=jnp.int32) - row_halo
    row_up = jnp.logical_not((inline_pos == inline_count - 1) & (own_row == width - 1))
    row_down = jnp.logical_not((inline_pos == 0) & (own_row == 0))
    own_col = jnp.arange(cols + 2 * col_halo, dtype=jnp.int32) - col_halo
    col_up = jnp.logical_not((xline_pos == xline_count - 1) & (own_col == cols - 1))
    col_down = jnp.logical_not((xline_pos == 0) & (own_col == 0))
    sample = jnp.arange(samples, dtype=jnp.int32)
    return [
        (row_up[:, None, None], row_down[:, None, None]),
        (col_up[None, :, None], col_down[None, :, None]),
        ((sample < samples - 1)[None, None, :], (sample > 0)[None, None, :]),
    ]


def relax_step(values, coeffs, masks):
    change = jnp.zeros_like(values)
    for which_axis in range(3):
        kk = coeffs[which_axis]
        up_open, down_open = masks[which_axis]
        for offset, opened in ((1, up_open), (-1, down_open)):
            change = change + 0.5 * (kk + neighbor(kk, which_axis, offset, opened)) * (
                neighbor(values, which_axis, offset, opened) - values
            )
    return values + step_size * change


def attributes(grown, masks):
    grads = []
    for which_axis in range(3):
        up_open, down_open = masks[which_axis]
        grads.append(
            0.5
            * (neighbor(grown, which_axis, 1, up_open) - neighbor(grown, which_axis, -1, down_open))
        )
    seconds = []
    for which_axis in range(2):
        up_open, down_open = masks[which_axis]
        seconds.append(
            neighbor(grown, which_axis, 1, up_open)
            + neighbor(grown, which_axis, -1, down_open)
            - 2.0 * grown
        )
    combos = [(0, 0), (1, 1), (2, 2), (0, 1), (0, 2), (1, 2)]
    tensor = jnp.stack(
        [grads[first_index] * grads[second_index] for first_index, second_index in combos], 0
    )
    for which_axis in range(3):
        up_open, down_open = masks[which_axis]
        tensor = 0.25 * (
            neighbor(tensor, which_axis + 1, 1, up_open)
            + 2.0 * tensor
            + neighbor(tensor, which_axis + 1, -1, down_open)
        )
    trace = tensor[0] + tensor[1] + tensor[2]
    minors = (
        tensor[0] * tensor[1]
        - tensor[3] * tensor[3]
        + tensor[0] * tensor[2]
        - tensor[4] * tensor[4]
        + tensor[1] * tensor[2]
        - tensor[5] * tensor[5]
    )
    coherence = 1.0 - 3.0 * minors / (trace * trace + epsilon)
    curvature = (seconds[0] + seconds[1]) / (1.0 + grads[0] * grads[0] + grads[1] * grads[1]) ** 1.5
    return coherence, curvature


def on_device(survey, conduct, widths):
    h = HALO
    batch = lax.axis_index("segment")
    field = lax.dynamic_index_in_dim(survey, batch, 0, keepdims=False)
    coeffs = lax.dynamic_index_in_dim(conduct, batch, 1, keepdims=False).astype(jnp.float32)
    width = lax.dynamic_index_in_dim(widths[:, 0], batch, 0, keepdims=False)
    rows, cols, samples = field.shape
    live = (jnp.arange(rows, dtype=jnp.int32) < width)[:, None, None]

    values = jnp.where(live, field, 0.0)
    wide = with_columns(jnp.concatenate([values[None], coeffs], 0), cols)
    grown = with_rows(wide, width, h)
    masks = face_masks(width, rows, cols, samples, h, cols)
    values, coeffs_grown = grown[0], grown[1:]
    for repeat in range(STEPS):
        values = relax_step(values, coeffs_grown, masks)
    smooth = values[h : h + rows, cols - h : 2 * cols + h]

    grown = with_rows(smooth, width, h)
    masks = face_masks(width, rows, cols, samples, h, h)
    coherence, curvature = attributes(grown, masks)
    outcome = jnp.stack([coherence, curvature], 0)[:, h : h + rows, h : h + cols]
    outcome = jnp.where(live[None], outcome, 0.0)
    return (outcome[0][None], outcome[1][None])


def solution(mesh):
    placed = (
        P(None, "inline", "xline", None),
        P(None, None, "inline", "xline", None),
        P(None, "inline"),
    )
    return jax.shard_map(
        on_device,
        mesh=mesh,
        in_specs=placed,
        out_specs=(P("segment", "inline", "xline", None), P("segment", "inline", "xline", None)),
        check_vma=False,
    )
```

```python
import jax
import jax.numpy as jnp
from jax import lax
from jax.sharding import PartitionSpec as P

STEPS = 2
HALO = 2


step_size = 0.15
epsilon = 1e-06


def shifted(source, which_axis, offset):
    length = source.shape[which_axis]
    margins = [(0, 0)] * source.ndim
    if offset > 0:
        margins[which_axis] = (0, offset)
        padded = jnp.pad(source, margins)
        return lax.slice_in_dim(padded, offset, offset + length, axis=which_axis)
    margins[which_axis] = (-offset, 0)
    padded = jnp.pad(source, margins)
    return lax.slice_in_dim(padded, 0, length, axis=which_axis)


def neighbor(source, which_axis, offset, opened):
    return jnp.where(opened, shifted(source, which_axis, offset), source)


def moved(value, d_inline, d_xline):
    n_i = lax.axis_size("inline")
    n_x = lax.axis_size("xline")
    if d_xline == 0:
        pairs = [(i, i + d_inline) for i in range(n_i) if 0 <= i + d_inline < n_i]
        return lax.ppermute(value, "inline", pairs)
    if d_inline == 0:
        pairs = [(x, x + d_xline) for x in range(n_x) if 0 <= x + d_xline < n_x]
        return lax.ppermute(value, "xline", pairs)
    pairs = []
    for i in range(n_i):
        for x in range(n_x):
            ti, tx = i + d_inline, x + d_xline
            if 0 <= ti < n_i and 0 <= tx < n_x:
                pairs.append((i * n_x + x, ti * n_x + tx))
    return lax.ppermute(value, ("inline", "xline"), pairs)


def with_columns(block, depth):
    ca = block.ndim - 2
    cols = block.shape[ca]
    from_left = moved(lax.slice_in_dim(block, cols - depth, cols, axis=ca), 0, 1)
    from_right = moved(lax.slice_in_dim(block, 0, depth, axis=ca), 0, -1)
    return jnp.concatenate([from_left, block, from_right], ca)


def with_rows(block, width, depth):
    ra = block.ndim - 3
    from_prev = moved(lax.dynamic_slice_in_dim(block, width - depth, depth, ra), 1, 0)
    from_next = moved(lax.slice_in_dim(block, 0, depth, axis=ra), -1, 0)
    return placed_rows(block, from_prev, from_next, width, depth)


def placed_rows(block, from_prev, from_next, width, depth):
    ra = block.ndim - 3
    stacked = jnp.concatenate([from_prev, block, jnp.zeros_like(from_next)], ra)
    return lax.dynamic_update_slice_in_dim(stacked, from_next, depth + width, ra)


def packed(pieces):
    samples = pieces[0].shape[-1]
    return jnp.concatenate([piece.reshape(-1, samples) for piece in pieces], 0)


def unpacked(flat, shapes):
    out, at = [], 0
    for shape in shapes:
        count = 1
        for size in shape[:-1]:
            count *= size
        out.append(flat[at : at + count].reshape(shape))
        at += count
    return out


def diffusion_columns(fields):
    n_f, rows, cols, samples = fields.shape
    far = jnp.stack([fields[0], fields[2]], 0)
    to_right = packed([fields[:, :, 1:], far[:, :, 0]])
    to_left = packed([fields[:, :, : cols - 1], far[:, :, cols - 1]])
    from_left = unpacked(moved(to_right, 0, 1), [(n_f, rows, cols - 1, samples), (2, rows, samples)])
    from_right = unpacked(moved(to_left, 0, -1), [(n_f, rows, cols - 1, samples), (2, rows, samples)])

    def edge(near, outer, outer_first):
        zero = jnp.zeros_like(outer[0])
        column = jnp.stack([outer[0], zero, outer[1], zero], 0)[:, :, None]
        parts = [column, near] if outer_first else [near, column]
        return jnp.concatenate(parts, 2)

    left = edge(from_left[0], from_left[1], True)
    right = edge(from_right[0], from_right[1], False)
    return jnp.concatenate([left, fields, right], 2)


def diffusion_rows(wide, width, cols):
    n_f, rows, n_c, samples = wide.shape
    h = HALO
    near = slice(cols - 3, 2 * cols + 3)
    mid = slice(cols - 2, 2 * cols + 2)

    def pieces(row_near, row_far):
        return packed([row_near[0:3, near], row_near[3, mid], row_far[0:2, mid]])

    last = lax.dynamic_slice_in_dim(wide, width - h, h, 1)
    to_next = pieces(last[:, 1], last[:, 0])
    to_prev = pieces(wide[:, 0], wide[:, 1])
    shapes = [(3, cols + 6, samples), (cols + 4, samples), (2, cols + 4, samples)]

    def rebuilt(flat):
        p_near, p_time, p_far = unpacked(flat, shapes)
        pad_near = [(0, 0), (cols - 3, cols - 3), (0, 0)]
        pad_mid = [(0, 0), (cols - 2, cols - 2), (0, 0)]
        row_near = jnp.concatenate([jnp.pad(p_near, pad_near), jnp.pad(p_time[None], pad_mid)], 0)
        row_far = jnp.pad(jnp.pad(p_far, pad_mid), [(0, 2), (0, 0), (0, 0)])
        return row_near, row_far

    prev_near, prev_far = rebuilt(moved(to_next, 1, 0))
    next_near, next_far = rebuilt(moved(to_prev, -1, 0))
    from_prev = jnp.stack([prev_far, prev_near], 1)
    from_next = jnp.stack([next_near, next_far], 1)
    return placed_rows(wide, from_prev, from_next, width, h)


def face_masks(width, rows, cols, samples, row_halo, col_halo):
    inline_pos = lax.axis_index("inline")
    inline_count = lax.axis_size("inline")
    xline_pos = lax.axis_index("xline")
    xline_count = lax.axis_size("xline")
    own_row = jnp.arange(rows + 2 * row_halo, dtype=jnp.int32) - row_halo
    row_up = jnp.logical_not((inline_pos == inline_count - 1) & (own_row == width - 1))
    row_down = jnp.logical_not((inline_pos == 0) & (own_row == 0))
    own_col = jnp.arange(cols + 2 * col_halo, dtype=jnp.int32) - col_halo
    col_up = jnp.logical_not((xline_pos == xline_count - 1) & (own_col == cols - 1))
    col_down = jnp.logical_not((xline_pos == 0) & (own_col == 0))
    sample = jnp.arange(samples, dtype=jnp.int32)
    return [
        (row_up[:, None, None], row_down[:, None, None]),
        (col_up[None, :, None], col_down[None, :, None]),
        ((sample < samples - 1)[None, None, :], (sample > 0)[None, None, :]),
    ]


def relax_step(values, coeffs, masks):
    change = jnp.zeros_like(values)
    for which_axis in range(3):
        kk = coeffs[which_axis]
        up_open, down_open = masks[which_axis]
        for offset, opened in ((1, up_open), (-1, down_open)):
            change = change + 0.5 * (kk + neighbor(kk, which_axis, offset, opened)) * (
                neighbor(values, which_axis, offset, opened) - values
            )
    return values + step_size * change


def attributes(grown, masks):
    grads = []
    for which_axis in range(3):
        up_open, down_open = masks[which_axis]
        grads.append(
            0.5
            * (neighbor(grown, which_axis, 1, up_open) - neighbor(grown, which_axis, -1, down_open))
        )
    seconds = []
    for which_axis in range(2):
        up_open, down_open = masks[which_axis]
        seconds.append(
            neighbor(grown, which_axis, 1, up_open)
            + neighbor(grown, which_axis, -1, down_open)
            - 2.0 * grown
        )
    combos = [(0, 0), (1, 1), (2, 2), (0, 1), (0, 2), (1, 2)]
    tensor = jnp.stack(
        [grads[first_index] * grads[second_index] for first_index, second_index in combos], 0
    )
    for which_axis in range(3):
        up_open, down_open = masks[which_axis]
        tensor = 0.25 * (
            neighbor(tensor, which_axis + 1, 1, up_open)
            + 2.0 * tensor
            + neighbor(tensor, which_axis + 1, -1, down_open)
        )
    trace = tensor[0] + tensor[1] + tensor[2]
    minors = (
        tensor[0] * tensor[1]
        - tensor[3] * tensor[3]
        + tensor[0] * tensor[2]
        - tensor[4] * tensor[4]
        + tensor[1] * tensor[2]
        - tensor[5] * tensor[5]
    )
    coherence = 1.0 - 3.0 * minors / (trace * trace + epsilon)
    curvature = (seconds[0] + seconds[1]) / (1.0 + grads[0] * grads[0] + grads[1] * grads[1]) ** 1.5
    return coherence, curvature


def on_device(survey, conduct, widths):
    h = HALO
    batch = lax.axis_index("segment")
    field = lax.dynamic_index_in_dim(survey, batch, 0, keepdims=False)
    coeffs = lax.dynamic_index_in_dim(conduct, batch, 1, keepdims=False).astype(jnp.float32)
    width = lax.dynamic_index_in_dim(widths[:, 0], batch, 0, keepdims=False)
    rows, cols, samples = field.shape
    live = (jnp.arange(rows, dtype=jnp.int32) < width)[:, None, None]

    values = jnp.where(live, field, 0.0)
    wide = diffusion_columns(jnp.concatenate([values[None], coeffs], 0))
    grown = diffusion_rows(wide, width, cols)
    masks = face_masks(width, rows, cols, samples, h, cols)
    values, coeffs_grown = grown[0], grown[1:]
    for repeat in range(STEPS):
        values = relax_step(values, coeffs_grown, masks)
    smooth = values[h : h + rows, cols - h : 2 * cols + h]

    grown = with_rows(smooth, width, h)
    masks = face_masks(width, rows, cols, samples, h, h)
    coherence, curvature = attributes(grown, masks)
    outcome = jnp.stack([coherence, curvature], 0)[:, h : h + rows, h : h + cols]
    outcome = jnp.where(live[None], outcome, 0.0)
    return (outcome[0][None], outcome[1][None])


def solution(mesh):
    placed = (
        P(None, "inline", "xline", None),
        P(None, None, "inline", "xline", None),
        P(None, "inline"),
    )
    return jax.shard_map(
        on_device,
        mesh=mesh,
        in_specs=placed,
        out_specs=(P("segment", "inline", "xline", None), P("segment", "inline", "xline", None)),
        check_vma=False,
    )
```

```python
import jax
import jax.numpy as jnp
from jax import lax
from jax.sharding import PartitionSpec as P

STEPS = 2
HALO = 2


step_size = 0.15
epsilon = 1e-06


def shifted(source, which_axis, offset):
    length = source.shape[which_axis]
    margins = [(0, 0)] * source.ndim
    if offset > 0:
        margins[which_axis] = (0, offset)
        padded = jnp.pad(source, margins)
        return lax.slice_in_dim(padded, offset, offset + length, axis=which_axis)
    margins[which_axis] = (-offset, 0)
    padded = jnp.pad(source, margins)
    return lax.slice_in_dim(padded, 0, length, axis=which_axis)


def neighbor(source, which_axis, offset, opened):
    return jnp.where(opened, shifted(source, which_axis, offset), source)


def moved(value, d_inline, d_xline):
    n_i = lax.axis_size("inline")
    n_x = lax.axis_size("xline")
    if d_xline == 0:
        pairs = [(i, i + d_inline) for i in range(n_i) if 0 <= i + d_inline < n_i]
        return lax.ppermute(value, "inline", pairs)
    if d_inline == 0:
        pairs = [(x, x + d_xline) for x in range(n_x) if 0 <= x + d_xline < n_x]
        return lax.ppermute(value, "xline", pairs)
    pairs = []
    for i in range(n_i):
        for x in range(n_x):
            ti, tx = i + d_inline, x + d_xline
            if 0 <= ti < n_i and 0 <= tx < n_x:
                pairs.append((i * n_x + x, ti * n_x + tx))
    return lax.ppermute(value, ("inline", "xline"), pairs)


def with_columns(block, depth):
    ca = block.ndim - 2
    cols = block.shape[ca]
    from_left = moved(lax.slice_in_dim(block, cols - depth, cols, axis=ca), 0, 1)
    from_right = moved(lax.slice_in_dim(block, 0, depth, axis=ca), 0, -1)
    return jnp.concatenate([from_left, block, from_right], ca)


def with_rows(block, width, depth):
    ra = block.ndim - 3
    from_prev = moved(lax.dynamic_slice_in_dim(block, width - depth, depth, ra), 1, 0)
    from_next = moved(lax.slice_in_dim(block, 0, depth, axis=ra), -1, 0)
    return placed_rows(block, from_prev, from_next, width, depth)


def placed_rows(block, from_prev, from_next, width, depth):
    ra = block.ndim - 3
    stacked = jnp.concatenate([from_prev, block, jnp.zeros_like(from_next)], ra)
    return lax.dynamic_update_slice_in_dim(stacked, from_next, depth + width, ra)


def packed(pieces):
    samples = pieces[0].shape[-1]
    return jnp.concatenate([piece.reshape(-1, samples) for piece in pieces], 0)


def unpacked(flat, shapes):
    out, at = [], 0
    for shape in shapes:
        count = 1
        for size in shape[:-1]:
            count *= size
        out.append(flat[at : at + count].reshape(shape))
        at += count
    return out


def diffusion_columns(fields):
    n_f, rows, cols, samples = fields.shape
    far = jnp.stack([fields[0], fields[2]], 0)
    to_right = packed([fields[:, :, 1:], far[:, :, 0]])
    to_left = packed([fields[:, :, : cols - 1], far[:, :, cols - 1]])
    position = lax.axis_index("xline")
    count = lax.axis_size("xline")
    chunks = jnp.stack(
        [
            jnp.where(j == position + 1, to_right, jnp.where(j == position - 1, to_left, 0.0))
            for j in range(count)
        ],
        0,
    )
    arrived = lax.all_to_all(chunks, "xline", 0, 0)
    shapes = [(n_f, rows, cols - 1, samples), (2, rows, samples)]
    from_left = unpacked(lax.dynamic_index_in_dim(arrived, jnp.maximum(position - 1, 0), 0, False), shapes)
    from_right = unpacked(
        lax.dynamic_index_in_dim(arrived, jnp.minimum(position + 1, count - 1), 0, False), shapes
    )

    def edge(near, outer, outer_first):
        zero = jnp.zeros_like(outer[0])
        column = jnp.stack([outer[0], zero, outer[1], zero], 0)[:, :, None]
        parts = [column, near] if outer_first else [near, column]
        return jnp.concatenate(parts, 2)

    left = edge(from_left[0], from_left[1], True)
    right = edge(from_right[0], from_right[1], False)
    return jnp.concatenate([left, fields, right], 2)


def diffusion_rows(wide, width, cols):
    n_f, rows, n_c, samples = wide.shape
    h = HALO
    near = slice(cols - 3, 2 * cols + 3)
    mid = slice(cols - 2, 2 * cols + 2)

    def pieces(row_near, row_far):
        return packed([row_near[0:3, near], row_near[3, mid], row_far[0:2, mid]])

    last = lax.dynamic_slice_in_dim(wide, width - h, h, 1)
    to_next = pieces(last[:, 1], last[:, 0])
    to_prev = pieces(wide[:, 0], wide[:, 1])
    shapes = [(3, cols + 6, samples), (cols + 4, samples), (2, cols + 4, samples)]

    def rebuilt(flat):
        p_near, p_time, p_far = unpacked(flat, shapes)
        pad_near = [(0, 0), (cols - 3, cols - 3), (0, 0)]
        pad_mid = [(0, 0), (cols - 2, cols - 2), (0, 0)]
        row_near = jnp.concatenate([jnp.pad(p_near, pad_near), jnp.pad(p_time[None], pad_mid)], 0)
        row_far = jnp.pad(jnp.pad(p_far, pad_mid), [(0, 2), (0, 0), (0, 0)])
        return row_near, row_far

    prev_near, prev_far = rebuilt(moved(to_next, 1, 0))
    next_near, next_far = rebuilt(moved(to_prev, -1, 0))
    from_prev = jnp.stack([prev_far, prev_near], 1)
    from_next = jnp.stack([next_near, next_far], 1)
    return placed_rows(wide, from_prev, from_next, width, h)


def face_masks(width, rows, cols, samples, row_halo, col_halo):
    inline_pos = lax.axis_index("inline")
    inline_count = lax.axis_size("inline")
    xline_pos = lax.axis_index("xline")
    xline_count = lax.axis_size("xline")
    own_row = jnp.arange(rows + 2 * row_halo, dtype=jnp.int32) - row_halo
    row_up = jnp.logical_not((inline_pos == inline_count - 1) & (own_row == width - 1))
    row_down = jnp.logical_not((inline_pos == 0) & (own_row == 0))
    own_col = jnp.arange(cols + 2 * col_halo, dtype=jnp.int32) - col_halo
    col_up = jnp.logical_not((xline_pos == xline_count - 1) & (own_col == cols - 1))
    col_down = jnp.logical_not((xline_pos == 0) & (own_col == 0))
    sample = jnp.arange(samples, dtype=jnp.int32)
    return [
        (row_up[:, None, None], row_down[:, None, None]),
        (col_up[None, :, None], col_down[None, :, None]),
        ((sample < samples - 1)[None, None, :], (sample > 0)[None, None, :]),
    ]


def relax_step(values, coeffs, masks):
    change = jnp.zeros_like(values)
    for which_axis in range(3):
        kk = coeffs[which_axis]
        up_open, down_open = masks[which_axis]
        for offset, opened in ((1, up_open), (-1, down_open)):
            change = change + 0.5 * (kk + neighbor(kk, which_axis, offset, opened)) * (
                neighbor(values, which_axis, offset, opened) - values
            )
    return values + step_size * change


def attributes(grown, masks):
    grads = []
    for which_axis in range(3):
        up_open, down_open = masks[which_axis]
        grads.append(
            0.5
            * (neighbor(grown, which_axis, 1, up_open) - neighbor(grown, which_axis, -1, down_open))
        )
    seconds = []
    for which_axis in range(2):
        up_open, down_open = masks[which_axis]
        seconds.append(
            neighbor(grown, which_axis, 1, up_open)
            + neighbor(grown, which_axis, -1, down_open)
            - 2.0 * grown
        )
    combos = [(0, 0), (1, 1), (2, 2), (0, 1), (0, 2), (1, 2)]
    tensor = jnp.stack(
        [grads[first_index] * grads[second_index] for first_index, second_index in combos], 0
    )
    for which_axis in range(3):
        up_open, down_open = masks[which_axis]
        tensor = 0.25 * (
            neighbor(tensor, which_axis + 1, 1, up_open)
            + 2.0 * tensor
            + neighbor(tensor, which_axis + 1, -1, down_open)
        )
    trace = tensor[0] + tensor[1] + tensor[2]
    minors = (
        tensor[0] * tensor[1]
        - tensor[3] * tensor[3]
        + tensor[0] * tensor[2]
        - tensor[4] * tensor[4]
        + tensor[1] * tensor[2]
        - tensor[5] * tensor[5]
    )
    coherence = 1.0 - 3.0 * minors / (trace * trace + epsilon)
    curvature = (seconds[0] + seconds[1]) / (1.0 + grads[0] * grads[0] + grads[1] * grads[1]) ** 1.5
    return coherence, curvature


def on_device(survey, conduct, widths):
    h = HALO
    batch = lax.axis_index("segment")
    field = lax.dynamic_index_in_dim(survey, batch, 0, keepdims=False)
    coeffs = lax.dynamic_index_in_dim(conduct, batch, 1, keepdims=False).astype(jnp.float32)
    width = lax.dynamic_index_in_dim(widths[:, 0], batch, 0, keepdims=False)
    rows, cols, samples = field.shape
    live = (jnp.arange(rows, dtype=jnp.int32) < width)[:, None, None]

    values = jnp.where(live, field, 0.0)
    wide = diffusion_columns(jnp.concatenate([values[None], coeffs], 0))
    grown = diffusion_rows(wide, width, cols)
    masks = face_masks(width, rows, cols, samples, h, cols)
    values, coeffs_grown = grown[0], grown[1:]
    for repeat in range(STEPS):
        values = relax_step(values, coeffs_grown, masks)
    smooth = values[h : h + rows, cols - h : 2 * cols + h]

    grown = with_rows(smooth, width, h)
    masks = face_masks(width, rows, cols, samples, h, h)
    coherence, curvature = attributes(grown, masks)
    outcome = jnp.stack([coherence, curvature], 0)[:, h : h + rows, h : h + cols]
    outcome = jnp.where(live[None], outcome, 0.0)
    return (outcome[0][None], outcome[1][None])


def solution(mesh):
    placed = (
        P(None, "inline", "xline", None),
        P(None, None, "inline", "xline", None),
        P(None, "inline"),
    )
    return jax.shard_map(
        on_device,
        mesh=mesh,
        in_specs=placed,
        out_specs=(P("segment", "inline", "xline", None), P("segment", "inline", "xline", None)),
        check_vma=False,
    )
```

```python
import jax
import jax.numpy as jnp
from jax import lax
from jax.sharding import PartitionSpec as P

STEPS = 2
HALO = 2


step_size = 0.15
epsilon = 1e-06


def shifted(source, which_axis, offset):
    length = source.shape[which_axis]
    margins = [(0, 0)] * source.ndim
    if offset > 0:
        margins[which_axis] = (0, offset)
        padded = jnp.pad(source, margins)
        return lax.slice_in_dim(padded, offset, offset + length, axis=which_axis)
    margins[which_axis] = (-offset, 0)
    padded = jnp.pad(source, margins)
    return lax.slice_in_dim(padded, 0, length, axis=which_axis)


def neighbor(source, which_axis, offset, opened):
    return jnp.where(opened, shifted(source, which_axis, offset), source)


def moved(value, d_inline, d_xline):
    n_i = lax.axis_size("inline")
    n_x = lax.axis_size("xline")
    if d_xline == 0:
        pairs = [(i, i + d_inline) for i in range(n_i) if 0 <= i + d_inline < n_i]
        return lax.ppermute(value, "inline", pairs)
    if d_inline == 0:
        pairs = [(x, x + d_xline) for x in range(n_x) if 0 <= x + d_xline < n_x]
        return lax.ppermute(value, "xline", pairs)
    pairs = []
    for i in range(n_i):
        for x in range(n_x):
            ti, tx = i + d_inline, x + d_xline
            if 0 <= ti < n_i and 0 <= tx < n_x:
                pairs.append((i * n_x + x, ti * n_x + tx))
    return lax.ppermute(value, ("inline", "xline"), pairs)


def with_columns(block, depth):
    ca = block.ndim - 2
    cols = block.shape[ca]
    from_left = moved(lax.slice_in_dim(block, cols - depth, cols, axis=ca), 0, 1)
    from_right = moved(lax.slice_in_dim(block, 0, depth, axis=ca), 0, -1)
    return jnp.concatenate([from_left, block, from_right], ca)


def with_rows(block, width, depth):
    ra = block.ndim - 3
    from_prev = moved(lax.dynamic_slice_in_dim(block, width - depth, depth, ra), 1, 0)
    from_next = moved(lax.slice_in_dim(block, 0, depth, axis=ra), -1, 0)
    return placed_rows(block, from_prev, from_next, width, depth)


def placed_rows(block, from_prev, from_next, width, depth):
    ra = block.ndim - 3
    stacked = jnp.concatenate([from_prev, block, jnp.zeros_like(from_next)], ra)
    return lax.dynamic_update_slice_in_dim(stacked, from_next, depth + width, ra)


def packed(pieces):
    samples = pieces[0].shape[-1]
    return jnp.concatenate([piece.reshape(-1, samples) for piece in pieces], 0)


def unpacked(flat, shapes):
    out, at = [], 0
    for shape in shapes:
        count = 1
        for size in shape[:-1]:
            count *= size
        out.append(flat[at : at + count].reshape(shape))
        at += count
    return out


def diffusion_columns(fields):
    n_f, rows, cols, samples = fields.shape
    far = jnp.stack([fields[0], fields[2]], 0)
    to_right = packed([fields[:, :, 1:], far[:, :, 0]])
    to_left = packed([fields[:, :, : cols - 1], far[:, :, cols - 1]])
    from_left = unpacked(moved(to_right, 0, 1), [(n_f, rows, cols - 1, samples), (2, rows, samples)])
    from_right = unpacked(moved(to_left, 0, -1), [(n_f, rows, cols - 1, samples), (2, rows, samples)])

    def edge(near, outer, outer_first):
        zero = jnp.zeros_like(outer[0])
        column = jnp.stack([outer[0], zero, outer[1], zero], 0)[:, :, None]
        parts = [column, near] if outer_first else [near, column]
        return jnp.concatenate(parts, 2)

    left = edge(from_left[0], from_left[1], True)
    right = edge(from_right[0], from_right[1], False)
    return jnp.concatenate([left, fields, right], 2)


def diffusion_rows(wide, width, cols):
    n_f, rows, n_c, samples = wide.shape
    h = HALO
    near = slice(cols - 3, 2 * cols + 3)
    mid = slice(cols - 2, 2 * cols + 2)

    def pieces(row_near, row_far):
        return packed([row_near[0:3, near], row_near[3, mid], row_far[0:2, mid]])

    last = lax.dynamic_slice_in_dim(wide, width - h, h, 1)
    to_next = pieces(last[:, 1], last[:, 0])
    to_prev = pieces(wide[:, 0], wide[:, 1])
    shapes = [(3, cols + 6, samples), (cols + 4, samples), (2, cols + 4, samples)]

    def rebuilt(flat):
        p_near, p_time, p_far = unpacked(flat, shapes)
        pad_near = [(0, 0), (cols - 3, cols - 3), (0, 0)]
        pad_mid = [(0, 0), (cols - 2, cols - 2), (0, 0)]
        row_near = jnp.concatenate([jnp.pad(p_near, pad_near), jnp.pad(p_time[None], pad_mid)], 0)
        row_far = jnp.pad(jnp.pad(p_far, pad_mid), [(0, 2), (0, 0), (0, 0)])
        return row_near, row_far

    prev_near, prev_far = rebuilt(moved(to_next, 1, 0))
    next_near, next_far = rebuilt(moved(to_prev, -1, 0))
    from_prev = jnp.stack([prev_far, prev_near], 1)
    from_next = jnp.stack([next_near, next_far], 1)
    return placed_rows(wide, from_prev, from_next, width, h)


def face_masks(width, rows, cols, samples, row_halo, col_halo):
    inline_pos = lax.axis_index("inline")
    inline_count = lax.axis_size("inline")
    xline_pos = lax.axis_index("xline")
    xline_count = lax.axis_size("xline")
    own_row = jnp.arange(rows + 2 * row_halo, dtype=jnp.int32) - row_halo
    row_up = jnp.logical_not((inline_pos == inline_count - 1) & (own_row == width - 1))
    row_down = jnp.logical_not((inline_pos == 0) & (own_row == 0))
    own_col = jnp.arange(cols + 2 * col_halo, dtype=jnp.int32) - col_halo
    col_up = jnp.logical_not((xline_pos == xline_count - 1) & (own_col == cols - 1))
    col_down = jnp.logical_not((xline_pos == 0) & (own_col == 0))
    sample = jnp.arange(samples, dtype=jnp.int32)
    return [
        (row_up[:, None, None], row_down[:, None, None]),
        (col_up[None, :, None], col_down[None, :, None]),
        ((sample < samples - 1)[None, None, :], (sample > 0)[None, None, :]),
    ]


def relax_step(values, coeffs, masks):
    change = jnp.zeros_like(values)
    for which_axis in range(3):
        kk = coeffs[which_axis]
        up_open, down_open = masks[which_axis]
        for offset, opened in ((1, up_open), (-1, down_open)):
            change = change + 0.5 * (kk + neighbor(kk, which_axis, offset, opened)) * (
                neighbor(values, which_axis, offset, opened) - values
            )
    return values + step_size * change


def attributes(grown, masks):
    grads = []
    for which_axis in range(3):
        up_open, down_open = masks[which_axis]
        grads.append(
            0.5
            * (neighbor(grown, which_axis, 1, up_open) - neighbor(grown, which_axis, -1, down_open))
        )
    seconds = []
    for which_axis in range(2):
        up_open, down_open = masks[which_axis]
        seconds.append(
            neighbor(grown, which_axis, 1, up_open)
            + neighbor(grown, which_axis, -1, down_open)
            - 2.0 * grown
        )
    combos = [(0, 0), (1, 1), (2, 2), (0, 1), (0, 2), (1, 2)]
    tensor = []
    for first_index, second_index in combos:
        member = grads[first_index] * grads[second_index]
        for which_axis in range(3):
            up_open, down_open = masks[which_axis]
            member = 0.25 * (
                neighbor(member, which_axis, 1, up_open)
                + 2.0 * member
                + neighbor(member, which_axis, -1, down_open)
            )
        tensor.append(member)
    trace = tensor[0] + tensor[1] + tensor[2]
    minors = (
        tensor[0] * tensor[1]
        - tensor[3] * tensor[3]
        + tensor[0] * tensor[2]
        - tensor[4] * tensor[4]
        + tensor[1] * tensor[2]
        - tensor[5] * tensor[5]
    )
    coherence = 1.0 - 3.0 * minors / (trace * trace + epsilon)
    curvature = (seconds[0] + seconds[1]) / (1.0 + grads[0] * grads[0] + grads[1] * grads[1]) ** 1.5
    return coherence, curvature


def on_device(survey, conduct, widths):
    h = HALO
    batch = lax.axis_index("segment")
    field = lax.dynamic_index_in_dim(survey, batch, 0, keepdims=False)
    coeffs = lax.dynamic_index_in_dim(conduct, batch, 1, keepdims=False).astype(jnp.float32)
    width = lax.dynamic_index_in_dim(widths[:, 0], batch, 0, keepdims=False)
    rows, cols, samples = field.shape
    live = (jnp.arange(rows, dtype=jnp.int32) < width)[:, None, None]

    wide = diffusion_columns(jnp.concatenate([field[None], coeffs], 0))
    grown = diffusion_rows(wide, width, cols)
    masks = face_masks(width, rows, cols, samples, h, cols)
    values, coeffs_grown = grown[0], grown[1:]
    for repeat in range(STEPS):
        values = relax_step(values, coeffs_grown, masks)
    smooth = values[h : h + rows, cols - h : 2 * cols + h]

    grown = with_rows(smooth, width, h)
    masks = face_masks(width, rows, cols, samples, h, h)
    results = attributes(grown, masks)
    return tuple(jnp.where(live, value[h : h + rows, h : h + cols], 0.0)[None] for value in results)


def solution(mesh):
    placed = (
        P(None, "inline", "xline", None),
        P(None, None, "inline", "xline", None),
        P(None, "inline"),
    )
    return jax.shard_map(
        on_device,
        mesh=mesh,
        in_specs=placed,
        out_specs=(P("segment", "inline", "xline", None), P("segment", "inline", "xline", None)),
        check_vma=False,
    )
```

```python
import jax
import jax.numpy as jnp
from jax import lax
from jax.experimental import pallas as pl
from jax.experimental.pallas import tpu as pltpu
from jax.sharding import PartitionSpec as P

STEPS = 2
HALO = 2


step_size = 0.15
epsilon = 1e-06


def shifted(source, which_axis, offset):
    length = source.shape[which_axis]
    margins = [(0, 0)] * source.ndim
    if offset > 0:
        margins[which_axis] = (0, offset)
        padded = jnp.pad(source, margins)
        return lax.slice_in_dim(padded, offset, offset + length, axis=which_axis)
    margins[which_axis] = (-offset, 0)
    padded = jnp.pad(source, margins)
    return lax.slice_in_dim(padded, 0, length, axis=which_axis)


def neighbor(source, which_axis, offset, opened):
    return jnp.where(opened, shifted(source, which_axis, offset), source)


def moved(value, d_inline, d_xline):
    n_i = lax.axis_size("inline")
    n_x = lax.axis_size("xline")
    if d_xline == 0:
        pairs = [(i, i + d_inline) for i in range(n_i) if 0 <= i + d_inline < n_i]
        return lax.ppermute(value, "inline", pairs)
    if d_inline == 0:
        pairs = [(x, x + d_xline) for x in range(n_x) if 0 <= x + d_xline < n_x]
        return lax.ppermute(value, "xline", pairs)
    pairs = []
    for i in range(n_i):
        for x in range(n_x):
            ti, tx = i + d_inline, x + d_xline
            if 0 <= ti < n_i and 0 <= tx < n_x:
                pairs.append((i * n_x + x, ti * n_x + tx))
    return lax.ppermute(value, ("inline", "xline"), pairs)


def with_columns(block, depth):
    ca = block.ndim - 2
    cols = block.shape[ca]
    from_left = moved(lax.slice_in_dim(block, cols - depth, cols, axis=ca), 0, 1)
    from_right = moved(lax.slice_in_dim(block, 0, depth, axis=ca), 0, -1)
    return jnp.concatenate([from_left, block, from_right], ca)


def with_rows(block, width, depth):
    ra = block.ndim - 3
    from_prev = moved(lax.dynamic_slice_in_dim(block, width - depth, depth, ra), 1, 0)
    from_next = moved(lax.slice_in_dim(block, 0, depth, axis=ra), -1, 0)
    return placed_rows(block, from_prev, from_next, width, depth)


def placed_rows(block, from_prev, from_next, width, depth):
    ra = block.ndim - 3
    stacked = jnp.concatenate([from_prev, block, jnp.zeros_like(from_next)], ra)
    return lax.dynamic_update_slice_in_dim(stacked, from_next, depth + width, ra)


def packed(pieces):
    samples = pieces[0].shape[-1]
    return jnp.concatenate([piece.reshape(-1, samples) for piece in pieces], 0)


def unpacked(flat, shapes):
    out, at = [], 0
    for shape in shapes:
        count = 1
        for size in shape[:-1]:
            count *= size
        out.append(flat[at : at + count].reshape(shape))
        at += count
    return out


def diffusion_columns(fields):
    n_f, rows, cols, samples = fields.shape
    far = jnp.stack([fields[0], fields[2]], 0)
    to_right = packed([fields[:, :, 1:], far[:, :, 0]])
    to_left = packed([fields[:, :, : cols - 1], far[:, :, cols - 1]])
    from_left = unpacked(moved(to_right, 0, 1), [(n_f, rows, cols - 1, samples), (2, rows, samples)])
    from_right = unpacked(moved(to_left, 0, -1), [(n_f, rows, cols - 1, samples), (2, rows, samples)])

    def edge(near, outer, outer_first):
        zero = jnp.zeros_like(outer[0])
        column = jnp.stack([outer[0], zero, outer[1], zero], 0)[:, :, None]
        parts = [column, near] if outer_first else [near, column]
        return jnp.concatenate(parts, 2)

    left = edge(from_left[0], from_left[1], True)
    right = edge(from_right[0], from_right[1], False)
    return jnp.concatenate([left, fields, right], 2)


def diffusion_rows(wide, width, cols):
    n_f, rows, n_c, samples = wide.shape
    h = HALO
    near = slice(cols - 3, 2 * cols + 3)
    mid = slice(cols - 2, 2 * cols + 2)

    def pieces(row_near, row_far):
        return packed([row_near[0:3, near], row_near[3, mid], row_far[0:2, mid]])

    last = lax.dynamic_slice_in_dim(wide, width - h, h, 1)
    to_next = pieces(last[:, 1], last[:, 0])
    to_prev = pieces(wide[:, 0], wide[:, 1])
    shapes = [(3, cols + 6, samples), (cols + 4, samples), (2, cols + 4, samples)]

    def rebuilt(flat):
        p_near, p_time, p_far = unpacked(flat, shapes)
        pad_near = [(0, 0), (cols - 3, cols - 3), (0, 0)]
        pad_mid = [(0, 0), (cols - 2, cols - 2), (0, 0)]
        row_near = jnp.concatenate([jnp.pad(p_near, pad_near), jnp.pad(p_time[None], pad_mid)], 0)
        row_far = jnp.pad(jnp.pad(p_far, pad_mid), [(0, 2), (0, 0), (0, 0)])
        return row_near, row_far

    prev_near, prev_far = rebuilt(moved(to_next, 1, 0))
    next_near, next_far = rebuilt(moved(to_prev, -1, 0))
    from_prev = jnp.stack([prev_far, prev_near], 1)
    from_next = jnp.stack([next_near, next_far], 1)
    return placed_rows(wide, from_prev, from_next, width, h)


def face_masks(width, rows, cols, samples, row_halo, col_halo):
    inline_pos = lax.axis_index("inline")
    inline_count = lax.axis_size("inline")
    xline_pos = lax.axis_index("xline")
    xline_count = lax.axis_size("xline")
    own_row = jnp.arange(rows + 2 * row_halo, dtype=jnp.int32) - row_halo
    row_up = jnp.logical_not((inline_pos == inline_count - 1) & (own_row == width - 1))
    row_down = jnp.logical_not((inline_pos == 0) & (own_row == 0))
    own_col = jnp.arange(cols + 2 * col_halo, dtype=jnp.int32) - col_halo
    col_up = jnp.logical_not((xline_pos == xline_count - 1) & (own_col == cols - 1))
    col_down = jnp.logical_not((xline_pos == 0) & (own_col == 0))
    sample = jnp.arange(samples, dtype=jnp.int32)
    return [
        (row_up[:, None, None], row_down[:, None, None]),
        (col_up[None, :, None], col_down[None, :, None]),
        ((sample < samples - 1)[None, None, :], (sample > 0)[None, None, :]),
    ]


def relax_step(values, coeffs, masks):
    change = jnp.zeros_like(values)
    for which_axis in range(3):
        kk = coeffs[which_axis]
        up_open, down_open = masks[which_axis]
        for offset, opened in ((1, up_open), (-1, down_open)):
            change = change + 0.5 * (kk + neighbor(kk, which_axis, offset, opened)) * (
                neighbor(values, which_axis, offset, opened) - values
            )
    return values + step_size * change


def attributes(grown, masks):
    grads = []
    for which_axis in range(3):
        up_open, down_open = masks[which_axis]
        grads.append(
            0.5
            * (neighbor(grown, which_axis, 1, up_open) - neighbor(grown, which_axis, -1, down_open))
        )
    seconds = []
    for which_axis in range(2):
        up_open, down_open = masks[which_axis]
        seconds.append(
            neighbor(grown, which_axis, 1, up_open)
            + neighbor(grown, which_axis, -1, down_open)
            - 2.0 * grown
        )
    combos = [(0, 0), (1, 1), (2, 2), (0, 1), (0, 2), (1, 2)]
    tensor = []
    for first_index, second_index in combos:
        member = grads[first_index] * grads[second_index]
        for which_axis in range(3):
            up_open, down_open = masks[which_axis]
            member = 0.25 * (
                neighbor(member, which_axis, 1, up_open)
                + 2.0 * member
                + neighbor(member, which_axis, -1, down_open)
            )
        tensor.append(member)
    trace = tensor[0] + tensor[1] + tensor[2]
    minors = (
        tensor[0] * tensor[1]
        - tensor[3] * tensor[3]
        + tensor[0] * tensor[2]
        - tensor[4] * tensor[4]
        + tensor[1] * tensor[2]
        - tensor[5] * tensor[5]
    )
    coherence = 1.0 - 3.0 * minors / (trace * trace + epsilon)
    curvature = (seconds[0] + seconds[1]) / (1.0 + grads[0] * grads[0] + grads[1] * grads[1]) ** 1.5
    return coherence, curvature


def attributes_kernel(flags_ref, grown_ref, coherence_ref, curvature_ref):
    h = HALO
    width = flags_ref[0]
    first_row, last_row = flags_ref[1] != 0, flags_ref[2] != 0
    first_col, last_col = flags_ref[3] != 0, flags_ref[4] != 0
    grown = grown_ref[...]
    n_rows, n_cols, samples = grown.shape
    cols = n_cols - 2 * h

    def masks_for(lo, hi):
        shape = (hi - lo, n_cols, samples)
        row = lax.broadcasted_iota(jnp.int32, shape, 0) + (lo - h)
        col = lax.broadcasted_iota(jnp.int32, shape, 1) - h
        sample = lax.broadcasted_iota(jnp.int32, shape, 2)
        return [
            (jnp.logical_not(last_row & (row == width - 1)), jnp.logical_not(first_row & (row == 0))),
            (jnp.logical_not(last_col & (col == cols - 1)), jnp.logical_not(first_col & (col == 0))),
            (sample < samples - 1, sample > 0),
        ]

    def near(source, lo, hi, at, which_axis, offset, opened):
        centre = source[lo - at : hi - at]
        if which_axis == 0:
            moved_rows = source[lo - at + offset : hi - at + offset]
        else:
            length = source.shape[which_axis]
            moved_rows = pltpu.roll(centre, (-offset) % length, which_axis)
        return jnp.where(opened, moved_rows, centre)

    lo, hi = 1, n_rows - 1
    masks = masks_for(lo, hi)
    grads = []
    for which_axis in range(3):
        up_open, down_open = masks[which_axis]
        grads.append(
            0.5
            * (
                near(grown, lo, hi, 0, which_axis, 1, up_open)
                - near(grown, lo, hi, 0, which_axis, -1, down_open)
            )
        )
    inner_lo, inner_hi = h, n_rows - h
    inner = masks_for(inner_lo, inner_hi)
    centre = grown[inner_lo:inner_hi]
    seconds = []
    for which_axis in range(2):
        up_open, down_open = inner[which_axis]
        seconds.append(
            near(grown, inner_lo, inner_hi, 0, which_axis, 1, up_open)
            + near(grown, inner_lo, inner_hi, 0, which_axis, -1, down_open)
            - 2.0 * centre
        )
    combos = [(0, 0), (1, 1), (2, 2), (0, 1), (0, 2), (1, 2)]
    tensor = []
    for first_index, second_index in combos:
        member = grads[first_index] * grads[second_index]
        up_open, down_open = inner[0]
        member = 0.25 * (
            near(member, inner_lo, inner_hi, lo, 0, 1, up_open)
            + 2.0 * member[inner_lo - lo : inner_hi - lo]
            + near(member, inner_lo, inner_hi, lo, 0, -1, down_open)
        )
        for which_axis in (1, 2):
            up_open, down_open = inner[which_axis]
            member = 0.25 * (
                near(member, inner_lo, inner_hi, inner_lo, which_axis, 1, up_open)
                + 2.0 * member
                + near(member, inner_lo, inner_hi, inner_lo, which_axis, -1, down_open)
            )
        tensor.append(member)
    trace = tensor[0] + tensor[1] + tensor[2]
    minors = (
        tensor[0] * tensor[1]
        - tensor[3] * tensor[3]
        + tensor[0] * tensor[2]
        - tensor[4] * tensor[4]
        + tensor[1] * tensor[2]
        - tensor[5] * tensor[5]
    )
    coherence = 1.0 - 3.0 * minors / (trace * trace + epsilon)
    g_in = grads[0][inner_lo - lo : inner_hi - lo]
    g_x = grads[1][inner_lo - lo : inner_hi - lo]
    curvature = (seconds[0] + seconds[1]) / (1.0 + g_in * g_in + g_x * g_x) ** 1.5
    out_shape = coherence_ref.shape
    live = lax.broadcasted_iota(jnp.int32, out_shape, 0) < width
    for value, out_ref in ((coherence, coherence_ref), (curvature, curvature_ref)):
        value = pltpu.roll(value, n_cols - h, 1)[:, :cols]
        out_ref[...] = jnp.where(live, value, 0.0)


def attributes_call(grown, flags, rows, cols):
    samples = grown.shape[-1]
    out = jax.ShapeDtypeStruct((rows, cols, samples), jnp.float32)
    return pl.pallas_call(
        attributes_kernel,
        out_shape=(out, out),
        in_specs=[
            pl.BlockSpec(memory_space=pltpu.SMEM),
            pl.BlockSpec(memory_space=pltpu.VMEM),
        ],
        out_specs=(pl.BlockSpec(memory_space=pltpu.VMEM), pl.BlockSpec(memory_space=pltpu.VMEM)),
    )(flags, grown)


def on_device(survey, conduct, widths):
    h = HALO
    batch = lax.axis_index("segment")
    field = lax.dynamic_index_in_dim(survey, batch, 0, keepdims=False)
    coeffs = lax.dynamic_index_in_dim(conduct, batch, 1, keepdims=False).astype(jnp.float32)
    width = lax.dynamic_index_in_dim(widths[:, 0], batch, 0, keepdims=False)
    rows, cols, samples = field.shape
    live = (jnp.arange(rows, dtype=jnp.int32) < width)[:, None, None]

    wide = diffusion_columns(jnp.concatenate([field[None], coeffs], 0))
    grown = diffusion_rows(wide, width, cols)
    masks = face_masks(width, rows, cols, samples, h, cols)
    values, coeffs_grown = grown[0], grown[1:]
    for repeat in range(STEPS):
        values = relax_step(values, coeffs_grown, masks)
    smooth = values[h : h + rows, cols - h : 2 * cols + h]

    grown = with_rows(smooth, width, h)
    masks = face_masks(width, rows, cols, samples, h, h)
    flags = jnp.stack(
        [
            width,
            (lax.axis_index("inline") == 0).astype(jnp.int32),
            (lax.axis_index("inline") == lax.axis_size("inline") - 1).astype(jnp.int32),
            (lax.axis_index("xline") == 0).astype(jnp.int32),
            (lax.axis_index("xline") == lax.axis_size("xline") - 1).astype(jnp.int32),
        ]
    )
    results = attributes_call(grown, flags, rows, cols)
    return tuple(value[None] for value in results)


def solution(mesh):
    placed = (
        P(None, "inline", "xline", None),
        P(None, None, "inline", "xline", None),
        P(None, "inline"),
    )
    return jax.shard_map(
        on_device,
        mesh=mesh,
        in_specs=placed,
        out_specs=(P("segment", "inline", "xline", None), P("segment", "inline", "xline", None)),
        check_vma=False,
    )
```

```python
import jax
import jax.numpy as jnp
from jax import lax
from jax.sharding import PartitionSpec as P

STEPS = 2
HALO = 2


step_size = 0.15
epsilon = 1e-06


def shifted(source, which_axis, offset):
    length = source.shape[which_axis]
    margins = [(0, 0)] * source.ndim
    if offset > 0:
        margins[which_axis] = (0, offset)
        padded = jnp.pad(source, margins)
        return lax.slice_in_dim(padded, offset, offset + length, axis=which_axis)
    margins[which_axis] = (-offset, 0)
    padded = jnp.pad(source, margins)
    return lax.slice_in_dim(padded, 0, length, axis=which_axis)


def neighbor(source, which_axis, offset, opened):
    return jnp.where(opened, shifted(source, which_axis, offset), source)


def moved(value, d_inline, d_xline):
    n_i = lax.axis_size("inline")
    n_x = lax.axis_size("xline")
    if d_xline == 0:
        pairs = [(i, i + d_inline) for i in range(n_i) if 0 <= i + d_inline < n_i]
        return lax.ppermute(value, "inline", pairs)
    if d_inline == 0:
        pairs = [(x, x + d_xline) for x in range(n_x) if 0 <= x + d_xline < n_x]
        return lax.ppermute(value, "xline", pairs)
    pairs = []
    for i in range(n_i):
        for x in range(n_x):
            ti, tx = i + d_inline, x + d_xline
            if 0 <= ti < n_i and 0 <= tx < n_x:
                pairs.append((i * n_x + x, ti * n_x + tx))
    return lax.ppermute(value, ("inline", "xline"), pairs)


def exchanged(to_next, to_prev, axis):
    count = lax.axis_size(axis)
    even = lax.axis_index(axis) % 2 == 0
    first = [(i, i ^ 1) for i in range(count) if i ^ 1 < count]
    second = [(i, j) for a in range(1, count - 1, 2) for i, j in ((a, a + 1), (a + 1, a))]
    got_first = lax.ppermute(jnp.where(even, to_next, to_prev), axis, first)
    got_second = lax.ppermute(jnp.where(even, to_prev, to_next), axis, second)
    return jnp.where(even, got_second, got_first), jnp.where(even, got_first, got_second)


def with_columns(block, depth):
    ca = block.ndim - 2
    cols = block.shape[ca]
    from_left = moved(lax.slice_in_dim(block, cols - depth, cols, axis=ca), 0, 1)
    from_right = moved(lax.slice_in_dim(block, 0, depth, axis=ca), 0, -1)
    return jnp.concatenate([from_left, block, from_right], ca)


def with_rows(block, width, depth):
    ra = block.ndim - 3
    from_prev, from_next = exchanged(
        lax.dynamic_slice_in_dim(block, width - depth, depth, ra), lax.slice_in_dim(block, 0, depth, axis=ra), "inline"
    )
    return placed_rows(block, from_prev, from_next, width, depth)


def placed_rows(block, from_prev, from_next, width, depth):
    ra = block.ndim - 3
    stacked = jnp.concatenate([from_prev, block, jnp.zeros_like(from_next)], ra)
    return lax.dynamic_update_slice_in_dim(stacked, from_next, depth + width, ra)


def packed(pieces):
    samples = pieces[0].shape[-1]
    return jnp.concatenate([piece.reshape(-1, samples) for piece in pieces], 0)


def unpacked(flat, shapes):
    out, at = [], 0
    for shape in shapes:
        count = 1
        for size in shape[:-1]:
            count *= size
        out.append(flat[at : at + count].reshape(shape))
        at += count
    return out


def diffusion_columns(fields):
    n_f, rows, cols, samples = fields.shape
    far = jnp.stack([fields[0], fields[2]], 0)
    to_right = packed([fields[:, :, 1:], far[:, :, 0]])
    to_left = packed([fields[:, :, : cols - 1], far[:, :, cols - 1]])
    got_left, got_right = exchanged(to_right, to_left, "xline")
    from_left = unpacked(got_left, [(n_f, rows, cols - 1, samples), (2, rows, samples)])
    from_right = unpacked(got_right, [(n_f, rows, cols - 1, samples), (2, rows, samples)])

    def edge(near, outer, outer_first):
        zero = jnp.zeros_like(outer[0])
        column = jnp.stack([outer[0], zero, outer[1], zero], 0)[:, :, None]
        parts = [column, near] if outer_first else [near, column]
        return jnp.concatenate(parts, 2)

    left = edge(from_left[0], from_left[1], True)
    right = edge(from_right[0], from_right[1], False)
    return jnp.concatenate([left, fields, right], 2)


def diffusion_rows(wide, width, cols):
    n_f, rows, n_c, samples = wide.shape
    h = HALO
    near = slice(cols - 3, 2 * cols + 3)
    mid = slice(cols - 2, 2 * cols + 2)

    def pieces(row_near, row_far):
        return packed([row_near[0:3, near], row_near[3, mid], row_far[0:2, mid]])

    last = lax.dynamic_slice_in_dim(wide, width - h, h, 1)
    to_next = pieces(last[:, 1], last[:, 0])
    to_prev = pieces(wide[:, 0], wide[:, 1])
    shapes = [(3, cols + 6, samples), (cols + 4, samples), (2, cols + 4, samples)]

    def rebuilt(flat):
        p_near, p_time, p_far = unpacked(flat, shapes)
        pad_near = [(0, 0), (cols - 3, cols - 3), (0, 0)]
        pad_mid = [(0, 0), (cols - 2, cols - 2), (0, 0)]
        row_near = jnp.concatenate([jnp.pad(p_near, pad_near), jnp.pad(p_time[None], pad_mid)], 0)
        row_far = jnp.pad(jnp.pad(p_far, pad_mid), [(0, 2), (0, 0), (0, 0)])
        return row_near, row_far

    got_prev, got_next = exchanged(to_next, to_prev, "inline")
    prev_near, prev_far = rebuilt(got_prev)
    next_near, next_far = rebuilt(got_next)
    from_prev = jnp.stack([prev_far, prev_near], 1)
    from_next = jnp.stack([next_near, next_far], 1)
    return placed_rows(wide, from_prev, from_next, width, h)


def face_masks(width, rows, cols, samples, row_halo, col_halo):
    inline_pos = lax.axis_index("inline")
    inline_count = lax.axis_size("inline")
    xline_pos = lax.axis_index("xline")
    xline_count = lax.axis_size("xline")
    own_row = jnp.arange(rows + 2 * row_halo, dtype=jnp.int32) - row_halo
    row_up = jnp.logical_not((inline_pos == inline_count - 1) & (own_row == width - 1))
    row_down = jnp.logical_not((inline_pos == 0) & (own_row == 0))
    own_col = jnp.arange(cols + 2 * col_halo, dtype=jnp.int32) - col_halo
    col_up = jnp.logical_not((xline_pos == xline_count - 1) & (own_col == cols - 1))
    col_down = jnp.logical_not((xline_pos == 0) & (own_col == 0))
    sample = jnp.arange(samples, dtype=jnp.int32)
    return [
        (row_up[:, None, None], row_down[:, None, None]),
        (col_up[None, :, None], col_down[None, :, None]),
        ((sample < samples - 1)[None, None, :], (sample > 0)[None, None, :]),
    ]


def relax_step(values, coeffs, masks):
    change = jnp.zeros_like(values)
    for which_axis in range(3):
        kk = coeffs[which_axis]
        up_open, down_open = masks[which_axis]
        for offset, opened in ((1, up_open), (-1, down_open)):
            change = change + 0.5 * (kk + neighbor(kk, which_axis, offset, opened)) * (
                neighbor(values, which_axis, offset, opened) - values
            )
    return values + step_size * change


def attributes(grown, masks):
    grads = []
    for which_axis in range(3):
        up_open, down_open = masks[which_axis]
        grads.append(
            0.5
            * (neighbor(grown, which_axis, 1, up_open) - neighbor(grown, which_axis, -1, down_open))
        )
    seconds = []
    for which_axis in range(2):
        up_open, down_open = masks[which_axis]
        seconds.append(
            neighbor(grown, which_axis, 1, up_open)
            + neighbor(grown, which_axis, -1, down_open)
            - 2.0 * grown
        )
    combos = [(0, 0), (1, 1), (2, 2), (0, 1), (0, 2), (1, 2)]
    tensor = []
    for first_index, second_index in combos:
        member = grads[first_index] * grads[second_index]
        for which_axis in range(3):
            up_open, down_open = masks[which_axis]
            member = 0.25 * (
                neighbor(member, which_axis, 1, up_open)
                + 2.0 * member
                + neighbor(member, which_axis, -1, down_open)
            )
        tensor.append(member)
    trace = tensor[0] + tensor[1] + tensor[2]
    minors = (
        tensor[0] * tensor[1]
        - tensor[3] * tensor[3]
        + tensor[0] * tensor[2]
        - tensor[4] * tensor[4]
        + tensor[1] * tensor[2]
        - tensor[5] * tensor[5]
    )
    coherence = 1.0 - 3.0 * minors / (trace * trace + epsilon)
    curvature = (seconds[0] + seconds[1]) / (1.0 + grads[0] * grads[0] + grads[1] * grads[1]) ** 1.5
    return coherence, curvature


def on_device(survey, conduct, widths):
    h = HALO
    batch = lax.axis_index("segment")
    field = lax.dynamic_index_in_dim(survey, batch, 0, keepdims=False)
    coeffs = lax.dynamic_index_in_dim(conduct, batch, 1, keepdims=False).astype(jnp.float32)
    width = lax.dynamic_index_in_dim(widths[:, 0], batch, 0, keepdims=False)
    rows, cols, samples = field.shape
    live = (jnp.arange(rows, dtype=jnp.int32) < width)[:, None, None]

    wide = diffusion_columns(jnp.concatenate([field[None], coeffs], 0))
    grown = diffusion_rows(wide, width, cols)
    masks = face_masks(width, rows, cols, samples, h, cols)
    values, coeffs_grown = grown[0], grown[1:]
    for repeat in range(STEPS):
        values = relax_step(values, coeffs_grown, masks)
    smooth = values[h : h + rows, cols - h : 2 * cols + h]

    grown = with_rows(smooth, width, h)
    masks = face_masks(width, rows, cols, samples, h, h)
    results = attributes(grown, masks)
    return tuple(jnp.where(live, value[h : h + rows, h : h + cols], 0.0)[None] for value in results)


def solution(mesh):
    placed = (
        P(None, "inline", "xline", None),
        P(None, None, "inline", "xline", None),
        P(None, "inline"),
    )
    return jax.shard_map(
        on_device,
        mesh=mesh,
        in_specs=placed,
        out_specs=(P("segment", "inline", "xline", None), P("segment", "inline", "xline", None)),
        check_vma=False,
    )
```

```python
import jax
import jax.numpy as jnp
from jax import lax
from jax.sharding import PartitionSpec as P

STEPS = 2
HALO = 2


step_size = 0.15
epsilon = 1e-06


def shifted(source, which_axis, offset):
    length = source.shape[which_axis]
    margins = [(0, 0)] * source.ndim
    if offset > 0:
        margins[which_axis] = (0, offset)
        padded = jnp.pad(source, margins)
        return lax.slice_in_dim(padded, offset, offset + length, axis=which_axis)
    margins[which_axis] = (-offset, 0)
    padded = jnp.pad(source, margins)
    return lax.slice_in_dim(padded, 0, length, axis=which_axis)


def neighbor(source, which_axis, offset, opened):
    return jnp.where(opened, shifted(source, which_axis, offset), source)


def moved(value, d_inline, d_xline):
    n_i = lax.axis_size("inline")
    n_x = lax.axis_size("xline")
    if d_xline == 0:
        pairs = [(i, i + d_inline) for i in range(n_i) if 0 <= i + d_inline < n_i]
        return lax.ppermute(value, "inline", pairs)
    if d_inline == 0:
        pairs = [(x, x + d_xline) for x in range(n_x) if 0 <= x + d_xline < n_x]
        return lax.ppermute(value, "xline", pairs)
    pairs = []
    for i in range(n_i):
        for x in range(n_x):
            ti, tx = i + d_inline, x + d_xline
            if 0 <= ti < n_i and 0 <= tx < n_x:
                pairs.append((i * n_x + x, ti * n_x + tx))
    return lax.ppermute(value, ("inline", "xline"), pairs)


def with_columns(block, depth):
    ca = block.ndim - 2
    cols = block.shape[ca]
    from_left = moved(lax.slice_in_dim(block, cols - depth, cols, axis=ca), 0, 1)
    from_right = moved(lax.slice_in_dim(block, 0, depth, axis=ca), 0, -1)
    return jnp.concatenate([from_left, block, from_right], ca)


def with_rows(block, width, depth):
    ra = block.ndim - 3
    from_prev = moved(lax.dynamic_slice_in_dim(block, width - depth, depth, ra), 1, 0)
    from_next = moved(lax.slice_in_dim(block, 0, depth, axis=ra), -1, 0)
    return placed_rows(block, from_prev, from_next, width, depth)


def placed_rows(block, from_prev, from_next, width, depth):
    ra = block.ndim - 3
    stacked = jnp.concatenate([from_prev, block, jnp.zeros_like(from_next)], ra)
    return lax.dynamic_update_slice_in_dim(stacked, from_next, depth + width, ra)


def packed(pieces):
    samples = pieces[0].shape[-1]
    return jnp.concatenate([piece.reshape(-1, samples) for piece in pieces], 0)


def unpacked(flat, shapes):
    out, at = [], 0
    for shape in shapes:
        count = 1
        for size in shape[:-1]:
            count *= size
        out.append(flat[at : at + count].reshape(shape))
        at += count
    return out


def diffusion_columns(fields):
    n_f, rows, cols, samples = fields.shape
    far = jnp.stack([fields[0], fields[2]], 0)
    to_right = packed([fields[:, :, 1:], far[:, :, 0]])
    to_left = packed([fields[:, :, : cols - 1], far[:, :, cols - 1]])
    from_left = unpacked(moved(to_right, 0, 1), [(n_f, rows, cols - 1, samples), (2, rows, samples)])
    from_right = unpacked(moved(to_left, 0, -1), [(n_f, rows, cols - 1, samples), (2, rows, samples)])

    def edge(near, outer, outer_first):
        zero = jnp.zeros_like(outer[0])
        column = jnp.stack([outer[0], zero, outer[1], zero], 0)[:, :, None]
        parts = [column, near] if outer_first else [near, column]
        return jnp.concatenate(parts, 2)

    left = edge(from_left[0], from_left[1], True)
    right = edge(from_right[0], from_right[1], False)
    return jnp.concatenate([left, fields, right], 2)


def diffusion_rows(wide, width, cols):
    n_f, rows, n_c, samples = wide.shape
    h = HALO
    near = slice(cols - 3, 2 * cols + 3)
    mid = slice(cols - 2, 2 * cols + 2)

    def pieces(row_near, row_far):
        return packed([row_near[0:3, near], row_near[3, mid], row_far[0:2, mid]])

    last = lax.dynamic_slice_in_dim(wide, width - h, h, 1)
    to_next = pieces(last[:, 1], last[:, 0])
    to_prev = pieces(wide[:, 0], wide[:, 1])
    shapes = [(3, cols + 6, samples), (cols + 4, samples), (2, cols + 4, samples)]

    def rebuilt(flat):
        p_near, p_time, p_far = unpacked(flat, shapes)
        pad_near = [(0, 0), (cols - 3, cols - 3), (0, 0)]
        pad_mid = [(0, 0), (cols - 2, cols - 2), (0, 0)]
        row_near = jnp.concatenate([jnp.pad(p_near, pad_near), jnp.pad(p_time[None], pad_mid)], 0)
        row_far = jnp.pad(jnp.pad(p_far, pad_mid), [(0, 2), (0, 0), (0, 0)])
        return row_near, row_far

    prev_near, prev_far = rebuilt(moved(to_next, 1, 0))
    next_near, next_far = rebuilt(moved(to_prev, -1, 0))
    from_prev = jnp.stack([prev_far, prev_near], 1)
    from_next = jnp.stack([next_near, next_far], 1)
    return placed_rows(wide, from_prev, from_next, width, h)


def face_masks(width, rows, cols, samples, row_halo, col_halo):
    inline_pos = lax.axis_index("inline")
    inline_count = lax.axis_size("inline")
    xline_pos = lax.axis_index("xline")
    xline_count = lax.axis_size("xline")
    own_row = jnp.arange(rows + 2 * row_halo, dtype=jnp.int32) - row_halo
    row_up = jnp.logical_not((inline_pos == inline_count - 1) & (own_row == width - 1))
    row_down = jnp.logical_not((inline_pos == 0) & (own_row == 0))
    own_col = jnp.arange(cols + 2 * col_halo, dtype=jnp.int32) - col_halo
    col_up = jnp.logical_not((xline_pos == xline_count - 1) & (own_col == cols - 1))
    col_down = jnp.logical_not((xline_pos == 0) & (own_col == 0))
    sample = jnp.arange(samples, dtype=jnp.int32)
    return [
        (row_up[:, None, None], row_down[:, None, None]),
        (col_up[None, :, None], col_down[None, :, None]),
        ((sample < samples - 1)[None, None, :], (sample > 0)[None, None, :]),
    ]


def near(source, lo, hi, at, which_axis, offset, opened):
    centre = source[lo - at : hi - at]
    if which_axis == 0:
        return jnp.where(opened, source[lo - at + offset : hi - at + offset], centre)
    return jnp.where(opened, shifted(centre, which_axis, offset), centre)


def rows_of(masks, lo, hi):
    rows = masks[0]
    return [(rows[0][lo:hi], rows[1][lo:hi])] + list(masks[1:])


def relax_rows(values, coeffs, masks, lo, hi, at):
    opened = rows_of(masks, lo, hi)
    centre = values[lo - at : hi - at]
    change = jnp.zeros_like(centre)
    for which_axis in range(3):
        kk = coeffs[which_axis]
        k_centre = kk[lo - at : hi - at]
        up_open, down_open = opened[which_axis]
        for offset, mask in ((1, up_open), (-1, down_open)):
            change = change + 0.5 * (k_centre + near(kk, lo, hi, at, which_axis, offset, mask)) * (
                near(values, lo, hi, at, which_axis, offset, mask) - centre
            )
    return centre + step_size * change


def attributes(grown, masks, h):
    n_rows = grown.shape[0]
    lo, hi = 1, n_rows - 1
    outer = rows_of(masks, lo, hi)
    grads = []
    for which_axis in range(3):
        up_open, down_open = outer[which_axis]
        grads.append(
            0.5
            * (
                near(grown, lo, hi, 0, which_axis, 1, up_open)
                - near(grown, lo, hi, 0, which_axis, -1, down_open)
            )
        )
    inner_lo, inner_hi = h, n_rows - h
    inner = rows_of(masks, inner_lo, inner_hi)
    centre = grown[inner_lo:inner_hi]
    seconds = []
    for which_axis in range(2):
        up_open, down_open = inner[which_axis]
        seconds.append(
            near(grown, inner_lo, inner_hi, 0, which_axis, 1, up_open)
            + near(grown, inner_lo, inner_hi, 0, which_axis, -1, down_open)
            - 2.0 * centre
        )
    combos = [(0, 0), (1, 1), (2, 2), (0, 1), (0, 2), (1, 2)]
    tensor = []
    for first_index, second_index in combos:
        member = grads[first_index] * grads[second_index]
        up_open, down_open = inner[0]
        member = 0.25 * (
            near(member, inner_lo, inner_hi, lo, 0, 1, up_open)
            + 2.0 * member[inner_lo - lo : inner_hi - lo]
            + near(member, inner_lo, inner_hi, lo, 0, -1, down_open)
        )
        for which_axis in (1, 2):
            up_open, down_open = inner[which_axis]
            member = 0.25 * (
                near(member, inner_lo, inner_hi, inner_lo, which_axis, 1, up_open)
                + 2.0 * member
                + near(member, inner_lo, inner_hi, inner_lo, which_axis, -1, down_open)
            )
        tensor.append(member)
    trace = tensor[0] + tensor[1] + tensor[2]
    minors = (
        tensor[0] * tensor[1]
        - tensor[3] * tensor[3]
        + tensor[0] * tensor[2]
        - tensor[4] * tensor[4]
        + tensor[1] * tensor[2]
        - tensor[5] * tensor[5]
    )
    coherence = 1.0 - 3.0 * minors / (trace * trace + epsilon)
    g_in = grads[0][inner_lo - lo : inner_hi - lo]
    g_x = grads[1][inner_lo - lo : inner_hi - lo]
    curvature = (seconds[0] + seconds[1]) / (1.0 + g_in * g_in + g_x * g_x) ** 1.5
    return coherence, curvature


def on_device(survey, conduct, widths):
    h = HALO
    batch = lax.axis_index("segment")
    field = lax.dynamic_index_in_dim(survey, batch, 0, keepdims=False)
    coeffs = lax.dynamic_index_in_dim(conduct, batch, 1, keepdims=False).astype(jnp.float32)
    width = lax.dynamic_index_in_dim(widths[:, 0], batch, 0, keepdims=False)
    rows, cols, samples = field.shape
    live = (jnp.arange(rows, dtype=jnp.int32) < width)[:, None, None]

    wide = diffusion_columns(jnp.concatenate([field[None], coeffs], 0))
    grown = diffusion_rows(wide, width, cols)
    masks = face_masks(width, rows, cols, samples, h, cols)
    values, coeffs_grown = grown[0], grown[1:]
    n_rows = values.shape[0]
    at = 0
    for repeat in range(STEPS):
        lo, hi = repeat + 1, n_rows - repeat - 1
        values = relax_rows(values, coeffs_grown[:, lo - 1 :], masks, lo, hi, at)
        at = lo
    smooth = values[h - at : h - at + rows, cols - h : 2 * cols + h]

    grown = with_rows(smooth, width, h)
    masks = face_masks(width, rows, cols, samples, h, h)
    results = attributes(grown, masks, h)
    return tuple(jnp.where(live, value[:, h : h + cols], 0.0)[None] for value in results)


def solution(mesh):
    placed = (
        P(None, "inline", "xline", None),
        P(None, None, "inline", "xline", None),
        P(None, "inline"),
    )
    return jax.shard_map(
        on_device,
        mesh=mesh,
        in_specs=placed,
        out_specs=(P("segment", "inline", "xline", None), P("segment", "inline", "xline", None)),
        check_vma=False,
    )
```

```python
import jax
import jax.numpy as jnp
from jax import lax
from jax.sharding import PartitionSpec as P

STEPS = 2
HALO = 2


step_size = 0.15
epsilon = 1e-06


def shifted(source, which_axis, offset):
    length = source.shape[which_axis]
    margins = [(0, 0)] * source.ndim
    if offset > 0:
        margins[which_axis] = (0, offset)
        padded = jnp.pad(source, margins)
        return lax.slice_in_dim(padded, offset, offset + length, axis=which_axis)
    margins[which_axis] = (-offset, 0)
    padded = jnp.pad(source, margins)
    return lax.slice_in_dim(padded, 0, length, axis=which_axis)


def neighbor(source, which_axis, offset, opened):
    return jnp.where(opened, shifted(source, which_axis, offset), source)


def moved(value, d_inline, d_xline):
    n_i = lax.axis_size("inline")
    n_x = lax.axis_size("xline")
    if d_xline == 0:
        pairs = [(i, i + d_inline) for i in range(n_i) if 0 <= i + d_inline < n_i]
        return lax.ppermute(value, "inline", pairs)
    if d_inline == 0:
        pairs = [(x, x + d_xline) for x in range(n_x) if 0 <= x + d_xline < n_x]
        return lax.ppermute(value, "xline", pairs)
    pairs = []
    for i in range(n_i):
        for x in range(n_x):
            ti, tx = i + d_inline, x + d_xline
            if 0 <= ti < n_i and 0 <= tx < n_x:
                pairs.append((i * n_x + x, ti * n_x + tx))
    return lax.ppermute(value, ("inline", "xline"), pairs)


def with_columns(block, depth):
    ca = block.ndim - 2
    cols = block.shape[ca]
    from_left = moved(lax.slice_in_dim(block, cols - depth, cols, axis=ca), 0, 1)
    from_right = moved(lax.slice_in_dim(block, 0, depth, axis=ca), 0, -1)
    return jnp.concatenate([from_left, block, from_right], ca)


def with_rows(block, width, depth):
    ra = block.ndim - 3
    from_prev = moved(lax.dynamic_slice_in_dim(block, width - depth, depth, ra), 1, 0)
    from_next = moved(lax.slice_in_dim(block, 0, depth, axis=ra), -1, 0)
    return placed_rows(block, from_prev, from_next, width, depth)


def placed_rows(block, from_prev, from_next, width, depth):
    ra = block.ndim - 3
    stacked = jnp.concatenate([from_prev, block, jnp.zeros_like(from_next)], ra)
    return lax.dynamic_update_slice_in_dim(stacked, from_next, depth + width, ra)


def packed(pieces):
    samples = pieces[0].shape[-1]
    return jnp.concatenate([piece.reshape(-1, samples) for piece in pieces], 0)


def unpacked(flat, shapes):
    out, at = [], 0
    for shape in shapes:
        count = 1
        for size in shape[:-1]:
            count *= size
        out.append(flat[at : at + count].reshape(shape))
        at += count
    return out


def diffusion_columns(fields):
    n_f, rows, cols, samples = fields.shape
    far = jnp.stack([fields[0], fields[2]], 0)
    to_right = packed([fields[:, :, 1:], far[:, :, 0]])
    to_left = packed([fields[:, :, : cols - 1], far[:, :, cols - 1]])
    from_left = unpacked(moved(to_right, 0, 1), [(n_f, rows, cols - 1, samples), (2, rows, samples)])
    from_right = unpacked(moved(to_left, 0, -1), [(n_f, rows, cols - 1, samples), (2, rows, samples)])

    def edge(near, outer, outer_first):
        zero = jnp.zeros_like(outer[0])
        column = jnp.stack([outer[0], zero, outer[1], zero], 0)[:, :, None]
        parts = [column, near] if outer_first else [near, column]
        return jnp.concatenate(parts, 2)

    left = edge(from_left[0], from_left[1], True)
    right = edge(from_right[0], from_right[1], False)
    return jnp.concatenate([left, fields, right], 2)


def diffusion_rows(wide, width, cols):
    n_f, rows, n_c, samples = wide.shape
    h = HALO
    near = slice(cols - 3, 2 * cols + 3)
    mid = slice(cols - 2, 2 * cols + 2)

    def pieces(row_near, row_far):
        return packed([row_near[0:3, near], row_near[3, mid], row_far[0:2, mid]])

    last = lax.dynamic_slice_in_dim(wide, width - h, h, 1)
    to_next = pieces(last[:, 1], last[:, 0])
    to_prev = pieces(wide[:, 0], wide[:, 1])
    shapes = [(3, cols + 6, samples), (cols + 4, samples), (2, cols + 4, samples)]

    def rebuilt(flat):
        p_near, p_time, p_far = unpacked(flat, shapes)
        pad_near = [(0, 0), (cols - 3, cols - 3), (0, 0)]
        pad_mid = [(0, 0), (cols - 2, cols - 2), (0, 0)]
        row_near = jnp.concatenate([jnp.pad(p_near, pad_near), jnp.pad(p_time[None], pad_mid)], 0)
        row_far = jnp.pad(jnp.pad(p_far, pad_mid), [(0, 2), (0, 0), (0, 0)])
        return row_near, row_far

    prev_near, prev_far = rebuilt(moved(to_next, 1, 0))
    next_near, next_far = rebuilt(moved(to_prev, -1, 0))
    from_prev = jnp.stack([prev_far, prev_near], 1)
    from_next = jnp.stack([next_near, next_far], 1)
    return placed_rows(wide, from_prev, from_next, width, h)


def face_masks(width, rows, cols, samples, row_halo, col_halo):
    inline_pos = lax.axis_index("inline")
    inline_count = lax.axis_size("inline")
    xline_pos = lax.axis_index("xline")
    xline_count = lax.axis_size("xline")
    own_row = jnp.arange(rows + 2 * row_halo, dtype=jnp.int32) - row_halo
    row_up = jnp.logical_not((inline_pos == inline_count - 1) & (own_row == width - 1))
    row_down = jnp.logical_not((inline_pos == 0) & (own_row == 0))
    own_col = jnp.arange(cols + 2 * col_halo, dtype=jnp.int32) - col_halo
    col_up = jnp.logical_not((xline_pos == xline_count - 1) & (own_col == cols - 1))
    col_down = jnp.logical_not((xline_pos == 0) & (own_col == 0))
    sample = jnp.arange(samples, dtype=jnp.int32)
    return [
        (row_up[:, None, None], row_down[:, None, None]),
        (col_up[None, :, None], col_down[None, :, None]),
        ((sample < samples - 1)[None, None, :], (sample > 0)[None, None, :]),
    ]


def near(source, lo, hi, at, which_axis, offset, opened):
    centre = source[lo - at : hi - at]
    if which_axis == 0:
        return jnp.where(opened, source[lo - at + offset : hi - at + offset], centre)
    return jnp.where(opened, shifted(centre, which_axis, offset), centre)


def rows_of(masks, lo, hi):
    rows = masks[0]
    return [(rows[0][lo:hi], rows[1][lo:hi])] + list(masks[1:])


def relax_rows(values, coeffs, masks, lo, hi, at):
    opened = rows_of(masks, lo, hi)
    centre = values[lo - at : hi - at]
    change = jnp.zeros_like(centre)
    for which_axis in range(3):
        kk = coeffs[which_axis]
        k_centre = kk[lo - at : hi - at]
        up_open, down_open = opened[which_axis]
        for offset, mask in ((1, up_open), (-1, down_open)):
            change = change + 0.5 * (k_centre + near(kk, lo, hi, at, which_axis, offset, mask)) * (
                near(values, lo, hi, at, which_axis, offset, mask) - centre
            )
    return centre + step_size * change


def attributes(grown, masks):
    grads = []
    for which_axis in range(3):
        up_open, down_open = masks[which_axis]
        grads.append(
            0.5
            * (neighbor(grown, which_axis, 1, up_open) - neighbor(grown, which_axis, -1, down_open))
        )
    seconds = []
    for which_axis in range(2):
        up_open, down_open = masks[which_axis]
        seconds.append(
            neighbor(grown, which_axis, 1, up_open)
            + neighbor(grown, which_axis, -1, down_open)
            - 2.0 * grown
        )
    combos = [(0, 0), (1, 1), (2, 2), (0, 1), (0, 2), (1, 2)]
    tensor = []
    for first_index, second_index in combos:
        member = grads[first_index] * grads[second_index]
        for which_axis in range(3):
            up_open, down_open = masks[which_axis]
            member = 0.25 * (
                neighbor(member, which_axis, 1, up_open)
                + 2.0 * member
                + neighbor(member, which_axis, -1, down_open)
            )
        tensor.append(member)
    trace = tensor[0] + tensor[1] + tensor[2]
    minors = (
        tensor[0] * tensor[1]
        - tensor[3] * tensor[3]
        + tensor[0] * tensor[2]
        - tensor[4] * tensor[4]
        + tensor[1] * tensor[2]
        - tensor[5] * tensor[5]
    )
    coherence = 1.0 - 3.0 * minors / (trace * trace + epsilon)
    curvature = (seconds[0] + seconds[1]) / (1.0 + grads[0] * grads[0] + grads[1] * grads[1]) ** 1.5
    return coherence, curvature


def on_device(survey, conduct, widths):
    h = HALO
    batch = lax.axis_index("segment")
    field = lax.dynamic_index_in_dim(survey, batch, 0, keepdims=False)
    coeffs = lax.dynamic_index_in_dim(conduct, batch, 1, keepdims=False).astype(jnp.float32)
    width = lax.dynamic_index_in_dim(widths[:, 0], batch, 0, keepdims=False)
    rows, cols, samples = field.shape
    live = (jnp.arange(rows, dtype=jnp.int32) < width)[:, None, None]

    wide = diffusion_columns(jnp.concatenate([field[None], coeffs], 0))
    grown = diffusion_rows(wide, width, cols)
    masks = face_masks(width, rows, cols, samples, h, cols)
    values, coeffs_grown = grown[0], grown[1:]
    n_rows = values.shape[0]
    at = 0
    for repeat in range(STEPS):
        lo, hi = repeat + 1, n_rows - repeat - 1
        values = relax_rows(values, coeffs_grown[:, lo - 1 :], masks, lo, hi, at)
        at = lo
    smooth = values[h - at : h - at + rows, cols - h : 2 * cols + h]

    grown = with_rows(smooth, width, h)
    masks = face_masks(width, rows, cols, samples, h, h)
    results = attributes(grown, masks)
    return tuple(jnp.where(live, value[h : h + rows, h : h + cols], 0.0)[None] for value in results)


def solution(mesh):
    placed = (
        P(None, "inline", "xline", None),
        P(None, None, "inline", "xline", None),
        P(None, "inline"),
    )
    return jax.shard_map(
        on_device,
        mesh=mesh,
        in_specs=placed,
        out_specs=(P("segment", "inline", "xline", None), P("segment", "inline", "xline", None)),
        check_vma=False,
    )
```

```python
import jax
import jax.numpy as jnp
from jax import lax
from jax.sharding import PartitionSpec as P

STEPS = 2
HALO = 2


step_size = 0.15
epsilon = 1e-06


def shifted(source, which_axis, offset):
    length = source.shape[which_axis]
    margins = [(0, 0)] * source.ndim
    if offset > 0:
        margins[which_axis] = (0, offset)
        padded = jnp.pad(source, margins)
        return lax.slice_in_dim(padded, offset, offset + length, axis=which_axis)
    margins[which_axis] = (-offset, 0)
    padded = jnp.pad(source, margins)
    return lax.slice_in_dim(padded, 0, length, axis=which_axis)


def neighbor(source, which_axis, offset, opened):
    return jnp.where(opened, shifted(source, which_axis, offset), source)


def moved(value, d_inline, d_xline):
    n_i = lax.axis_size("inline")
    n_x = lax.axis_size("xline")
    if d_xline == 0:
        pairs = [(i, i + d_inline) for i in range(n_i) if 0 <= i + d_inline < n_i]
        return lax.ppermute(value, "inline", pairs)
    if d_inline == 0:
        pairs = [(x, x + d_xline) for x in range(n_x) if 0 <= x + d_xline < n_x]
        return lax.ppermute(value, "xline", pairs)
    pairs = []
    for i in range(n_i):
        for x in range(n_x):
            ti, tx = i + d_inline, x + d_xline
            if 0 <= ti < n_i and 0 <= tx < n_x:
                pairs.append((i * n_x + x, ti * n_x + tx))
    return lax.ppermute(value, ("inline", "xline"), pairs)


def with_columns(block, depth):
    ca = block.ndim - 2
    cols = block.shape[ca]
    from_left = moved(lax.slice_in_dim(block, cols - depth, cols, axis=ca), 0, 1)
    from_right = moved(lax.slice_in_dim(block, 0, depth, axis=ca), 0, -1)
    return jnp.concatenate([from_left, block, from_right], ca)


def with_rows(block, width, depth):
    ra = block.ndim - 3
    from_prev = moved(lax.dynamic_slice_in_dim(block, width - depth, depth, ra), 1, 0)
    from_next = moved(lax.slice_in_dim(block, 0, depth, axis=ra), -1, 0)
    return placed_rows(block, from_prev, from_next, width, depth)


def placed_rows(block, from_prev, from_next, width, depth):
    ra = block.ndim - 3
    stacked = jnp.concatenate([from_prev, block, jnp.zeros_like(from_next)], ra)
    return lax.dynamic_update_slice_in_dim(stacked, from_next, depth + width, ra)


def packed(pieces):
    samples = pieces[0].shape[-1]
    return jnp.concatenate([piece.reshape(-1, samples) for piece in pieces], 0)


def unpacked(flat, shapes):
    out, at = [], 0
    for shape in shapes:
        count = 1
        for size in shape[:-1]:
            count *= size
        out.append(flat[at : at + count].reshape(shape))
        at += count
    return out


def diffusion_columns(fields):
    n_f, rows, cols, samples = fields.shape
    far = jnp.stack([fields[0], fields[2]], 0)
    to_right = packed([fields[:, :, 1:], far[:, :, 0]])
    to_left = packed([fields[:, :, : cols - 1], far[:, :, cols - 1]])
    from_left = unpacked(moved(to_right, 0, 1), [(n_f, rows, cols - 1, samples), (2, rows, samples)])
    from_right = unpacked(moved(to_left, 0, -1), [(n_f, rows, cols - 1, samples), (2, rows, samples)])

    def edge(near, outer, outer_first):
        zero = jnp.zeros_like(outer[0])
        column = jnp.stack([outer[0], zero, outer[1], zero], 0)[:, :, None]
        parts = [column, near] if outer_first else [near, column]
        return jnp.concatenate(parts, 2)

    left = edge(from_left[0], from_left[1], True)
    right = edge(from_right[0], from_right[1], False)
    return jnp.concatenate([left, fields, right], 2)


def diffusion_rows(wide, width, cols):
    n_f, rows, n_c, samples = wide.shape
    h = HALO
    near = slice(cols - 3, 2 * cols + 3)
    mid = slice(cols - 2, 2 * cols + 2)

    def pieces(row_near, row_far):
        return packed([row_near[0:3, near], row_near[3, mid], row_far[0:2, mid]])

    last = lax.dynamic_slice_in_dim(wide, width - h, h, 1)
    to_next = pieces(last[:, 1], last[:, 0])
    to_prev = pieces(wide[:, 0], wide[:, 1])
    shapes = [(3, cols + 6, samples), (cols + 4, samples), (2, cols + 4, samples)]

    def rebuilt(flat):
        p_near, p_time, p_far = unpacked(flat, shapes)
        pad_near = [(0, 0), (cols - 3, cols - 3), (0, 0)]
        pad_mid = [(0, 0), (cols - 2, cols - 2), (0, 0)]
        row_near = jnp.concatenate([jnp.pad(p_near, pad_near), jnp.pad(p_time[None], pad_mid)], 0)
        row_far = jnp.pad(jnp.pad(p_far, pad_mid), [(0, 2), (0, 0), (0, 0)])
        return row_near, row_far

    prev_near, prev_far = rebuilt(moved(to_next, 1, 0))
    next_near, next_far = rebuilt(moved(to_prev, -1, 0))
    from_prev = jnp.stack([prev_far, prev_near], 1)
    from_next = jnp.stack([next_near, next_far], 1)
    return placed_rows(wide, from_prev, from_next, width, h)


def face_masks(width, rows, cols, samples, row_halo, col_halo):
    inline_pos = lax.axis_index("inline")
    inline_count = lax.axis_size("inline")
    xline_pos = lax.axis_index("xline")
    xline_count = lax.axis_size("xline")
    own_row = jnp.arange(rows + 2 * row_halo, dtype=jnp.int32) - row_halo
    row_up = jnp.logical_not((inline_pos == inline_count - 1) & (own_row == width - 1))
    row_down = jnp.logical_not((inline_pos == 0) & (own_row == 0))
    own_col = jnp.arange(cols + 2 * col_halo, dtype=jnp.int32) - col_halo
    col_up = jnp.logical_not((xline_pos == xline_count - 1) & (own_col == cols - 1))
    col_down = jnp.logical_not((xline_pos == 0) & (own_col == 0))
    sample = jnp.arange(samples, dtype=jnp.int32)
    return [
        (row_up[:, None, None], row_down[:, None, None]),
        (col_up[None, :, None], col_down[None, :, None]),
        ((sample < samples - 1)[None, None, :], (sample > 0)[None, None, :]),
    ]


def near(source, lo, hi, at, which_axis, offset, opened):
    centre = source[lo - at : hi - at]
    if which_axis == 0:
        return jnp.where(opened, source[lo - at + offset : hi - at + offset], centre)
    return jnp.where(opened, shifted(centre, which_axis, offset), centre)


def rows_of(masks, lo, hi):
    rows = masks[0]
    return [(rows[0][lo:hi], rows[1][lo:hi])] + list(masks[1:])


def relax_rows(values, coeffs, masks, lo, hi, at):
    opened = rows_of(masks, lo, hi)
    centre = values[lo - at : hi - at]
    change = jnp.zeros_like(centre)
    for which_axis in range(3):
        kk = coeffs[which_axis]
        k_centre = kk[lo - at : hi - at]
        up_open, down_open = opened[which_axis]
        for offset, mask in ((1, up_open), (-1, down_open)):
            change = change + 0.5 * (k_centre + near(kk, lo, hi, at, which_axis, offset, mask)) * (
                near(values, lo, hi, at, which_axis, offset, mask) - centre
            )
    return centre + step_size * change


def attributes(grown, masks):
    grads = []
    for which_axis in range(3):
        up_open, down_open = masks[which_axis]
        grads.append(
            0.5
            * (neighbor(grown, which_axis, 1, up_open) - neighbor(grown, which_axis, -1, down_open))
        )
    seconds = []
    for which_axis in range(2):
        up_open, down_open = masks[which_axis]
        seconds.append(
            neighbor(grown, which_axis, 1, up_open)
            + neighbor(grown, which_axis, -1, down_open)
            - 2.0 * grown
        )
    combos = [(0, 0), (1, 1), (2, 2), (0, 1), (0, 2), (1, 2)]
    tensor = []
    for first_index, second_index in combos:
        member = grads[first_index] * grads[second_index]
        for which_axis in range(3):
            up_open, down_open = masks[which_axis]
            member = 0.25 * (
                neighbor(member, which_axis, 1, up_open)
                + 2.0 * member
                + neighbor(member, which_axis, -1, down_open)
            )
        tensor.append(member)
    trace = tensor[0] + tensor[1] + tensor[2]
    minors = (
        tensor[0] * tensor[1]
        - tensor[3] * tensor[3]
        + tensor[0] * tensor[2]
        - tensor[4] * tensor[4]
        + tensor[1] * tensor[2]
        - tensor[5] * tensor[5]
    )
    coherence = 1.0 - 3.0 * minors / (trace * trace + epsilon)
    curvature = (seconds[0] + seconds[1]) / (1.0 + grads[0] * grads[0] + grads[1] * grads[1]) ** 1.5
    return coherence, curvature


def on_device(survey, conduct, widths):
    h = HALO
    batch = lax.axis_index("segment")
    field = lax.optimization_barrier(lax.dynamic_index_in_dim(survey, batch, 0, keepdims=False))
    coeffs = lax.dynamic_index_in_dim(conduct, batch, 1, keepdims=False).astype(jnp.float32)
    width = lax.dynamic_index_in_dim(widths[:, 0], batch, 0, keepdims=False)
    rows, cols, samples = field.shape
    live = (jnp.arange(rows, dtype=jnp.int32) < width)[:, None, None]

    wide = diffusion_columns(jnp.concatenate([field[None], coeffs], 0))
    grown = diffusion_rows(wide, width, cols)
    masks = face_masks(width, rows, cols, samples, h, cols)
    values, coeffs_grown = grown[0], grown[1:]
    n_rows = values.shape[0]
    at = 0
    for repeat in range(STEPS):
        lo, hi = repeat + 1, n_rows - repeat - 1
        values = relax_rows(values, coeffs_grown[:, lo - 1 :], masks, lo, hi, at)
        at = lo
    smooth = values[h - at : h - at + rows, cols - h : 2 * cols + h]

    grown = with_rows(smooth, width, h)
    masks = face_masks(width, rows, cols, samples, h, h)
    results = attributes(grown, masks)
    return tuple(jnp.where(live, value[h : h + rows, h : h + cols], 0.0)[None] for value in results)


def solution(mesh):
    placed = (
        P(None, "inline", "xline", None),
        P(None, None, "inline", "xline", None),
        P(None, "inline"),
    )
    return jax.shard_map(
        on_device,
        mesh=mesh,
        in_specs=placed,
        out_specs=(P("segment", "inline", "xline", None), P("segment", "inline", "xline", None)),
        check_vma=False,
    )
```

```python
import jax
import jax.numpy as jnp
from jax import lax
from jax.sharding import PartitionSpec as P

STEPS = 2
HALO = 2


step_size = 0.15
epsilon = 1e-06


def shifted(source, which_axis, offset):
    length = source.shape[which_axis]
    margins = [(0, 0)] * source.ndim
    if offset > 0:
        margins[which_axis] = (0, offset)
        padded = jnp.pad(source, margins)
        return lax.slice_in_dim(padded, offset, offset + length, axis=which_axis)
    margins[which_axis] = (-offset, 0)
    padded = jnp.pad(source, margins)
    return lax.slice_in_dim(padded, 0, length, axis=which_axis)


def neighbor(source, which_axis, offset, opened):
    return jnp.where(opened, shifted(source, which_axis, offset), source)


def moved(value, d_inline, d_xline):
    n_i = lax.axis_size("inline")
    n_x = lax.axis_size("xline")
    if d_xline == 0:
        pairs = [(i, i + d_inline) for i in range(n_i) if 0 <= i + d_inline < n_i]
        return lax.ppermute(value, "inline", pairs)
    if d_inline == 0:
        pairs = [(x, x + d_xline) for x in range(n_x) if 0 <= x + d_xline < n_x]
        return lax.ppermute(value, "xline", pairs)
    pairs = []
    for i in range(n_i):
        for x in range(n_x):
            ti, tx = i + d_inline, x + d_xline
            if 0 <= ti < n_i and 0 <= tx < n_x:
                pairs.append((i * n_x + x, ti * n_x + tx))
    return lax.ppermute(value, ("inline", "xline"), pairs)


def with_columns(block, depth):
    ca = block.ndim - 2
    cols = block.shape[ca]
    from_left = moved(lax.slice_in_dim(block, cols - depth, cols, axis=ca), 0, 1)
    from_right = moved(lax.slice_in_dim(block, 0, depth, axis=ca), 0, -1)
    return jnp.concatenate([from_left, block, from_right], ca)


def with_rows(block, width, depth):
    ra = block.ndim - 3
    from_prev = moved(lax.dynamic_slice_in_dim(block, width - depth, depth, ra), 1, 0)
    from_next = moved(lax.slice_in_dim(block, 0, depth, axis=ra), -1, 0)
    return placed_rows(block, from_prev, from_next, width, depth)


def placed_rows(block, from_prev, from_next, width, depth):
    ra = block.ndim - 3
    stacked = jnp.concatenate([from_prev, block, jnp.zeros_like(from_next)], ra)
    return lax.dynamic_update_slice_in_dim(stacked, from_next, depth + width, ra)


def packed(pieces):
    samples = pieces[0].shape[-1]
    return jnp.concatenate([piece.reshape(-1, samples) for piece in pieces], 0)


def unpacked(flat, shapes):
    out, at = [], 0
    for shape in shapes:
        count = 1
        for size in shape[:-1]:
            count *= size
        out.append(flat[at : at + count].reshape(shape))
        at += count
    return out


def diffusion_columns(fields):
    n_f, rows, cols, samples = fields.shape
    far = jnp.stack([fields[0], fields[2]], 0)
    to_right = packed([fields[:, :, 1:], far[:, :, 0]])
    to_left = packed([fields[:, :, : cols - 1], far[:, :, cols - 1]])
    from_left = unpacked(moved(to_right, 0, 1), [(n_f, rows, cols - 1, samples), (2, rows, samples)])
    from_right = unpacked(moved(to_left, 0, -1), [(n_f, rows, cols - 1, samples), (2, rows, samples)])

    def edge(near, outer, outer_first):
        zero = jnp.zeros_like(outer[0])
        column = jnp.stack([outer[0], zero, outer[1], zero], 0)[:, :, None]
        parts = [column, near] if outer_first else [near, column]
        return jnp.concatenate(parts, 2)

    left = edge(from_left[0], from_left[1], True)
    right = edge(from_right[0], from_right[1], False)
    return jnp.concatenate([left, fields, right], 2)


def diffusion_rows(wide, width, cols):
    n_f, rows, n_c, samples = wide.shape
    h = HALO
    near = slice(cols - 3, 2 * cols + 3)
    mid = slice(cols - 2, 2 * cols + 2)

    def pieces(row_near, row_far):
        return packed([row_near[0:3, near], row_near[3, mid], row_far[0:2, mid]])

    last = lax.dynamic_slice_in_dim(wide, width - h, h, 1)
    to_next = pieces(last[:, 1], last[:, 0])
    to_prev = pieces(wide[:, 0], wide[:, 1])
    shapes = [(3, cols + 6, samples), (cols + 4, samples), (2, cols + 4, samples)]

    def rebuilt(flat):
        p_near, p_time, p_far = unpacked(flat, shapes)
        pad_near = [(0, 0), (cols - 3, cols - 3), (0, 0)]
        pad_mid = [(0, 0), (cols - 2, cols - 2), (0, 0)]
        row_near = jnp.concatenate([jnp.pad(p_near, pad_near), jnp.pad(p_time[None], pad_mid)], 0)
        row_far = jnp.pad(jnp.pad(p_far, pad_mid), [(0, 2), (0, 0), (0, 0)])
        return row_near, row_far

    prev_near, prev_far = rebuilt(moved(to_next, 1, 0))
    next_near, next_far = rebuilt(moved(to_prev, -1, 0))
    from_prev = jnp.stack([prev_far, prev_near], 1)
    from_next = jnp.stack([next_near, next_far], 1)
    return placed_rows(wide, from_prev, from_next, width, h)


def face_masks(width, rows, cols, samples, row_halo, col_halo):
    inline_pos = lax.axis_index("inline")
    inline_count = lax.axis_size("inline")
    xline_pos = lax.axis_index("xline")
    xline_count = lax.axis_size("xline")
    own_row = jnp.arange(rows + 2 * row_halo, dtype=jnp.int32) - row_halo
    row_up = jnp.logical_not((inline_pos == inline_count - 1) & (own_row == width - 1))
    row_down = jnp.logical_not((inline_pos == 0) & (own_row == 0))
    own_col = jnp.arange(cols + 2 * col_halo, dtype=jnp.int32) - col_halo
    col_up = jnp.logical_not((xline_pos == xline_count - 1) & (own_col == cols - 1))
    col_down = jnp.logical_not((xline_pos == 0) & (own_col == 0))
    sample = jnp.arange(samples, dtype=jnp.int32)
    return [
        (row_up[:, None, None], row_down[:, None, None]),
        (col_up[None, :, None], col_down[None, :, None]),
        ((sample < samples - 1)[None, None, :], (sample > 0)[None, None, :]),
    ]


def near(source, lo, hi, at, which_axis, offset, opened):
    centre = source[lo - at : hi - at]
    if which_axis == 0:
        return jnp.where(opened, source[lo - at + offset : hi - at + offset], centre)
    return jnp.where(opened, shifted(centre, which_axis, offset), centre)


def rows_of(masks, lo, hi):
    rows = masks[0]
    return [(rows[0][lo:hi], rows[1][lo:hi])] + list(masks[1:])


def relax_rows(values, coeffs, masks, lo, hi, at):
    opened = rows_of(masks, lo, hi)
    centre = values[lo - at : hi - at]
    change = jnp.zeros_like(centre)
    for which_axis in range(3):
        kk = coeffs[which_axis]
        k_centre = kk[lo - at : hi - at]
        up_open, down_open = opened[which_axis]
        for offset, mask in ((1, up_open), (-1, down_open)):
            change = change + 0.5 * (k_centre + near(kk, lo, hi, at, which_axis, offset, mask)) * (
                near(values, lo, hi, at, which_axis, offset, mask) - centre
            )
    return centre + step_size * change


def attributes(grown, masks):
    grads = []
    for which_axis in range(3):
        up_open, down_open = masks[which_axis]
        grads.append(
            0.5
            * (neighbor(grown, which_axis, 1, up_open) - neighbor(grown, which_axis, -1, down_open))
        )
    seconds = []
    for which_axis in range(2):
        up_open, down_open = masks[which_axis]
        seconds.append(
            neighbor(grown, which_axis, 1, up_open)
            + neighbor(grown, which_axis, -1, down_open)
            - 2.0 * grown
        )
    combos = [(0, 0), (1, 1), (2, 2), (0, 1), (0, 2), (1, 2)]
    tensor = []
    for first_index, second_index in combos:
        member = grads[first_index] * grads[second_index]
        for which_axis in range(3):
            up_open, down_open = masks[which_axis]
            member = 0.25 * (
                neighbor(member, which_axis, 1, up_open)
                + 2.0 * member
                + neighbor(member, which_axis, -1, down_open)
            )
        tensor.append(member)
    trace = tensor[0] + tensor[1] + tensor[2]
    minors = (
        tensor[0] * tensor[1]
        - tensor[3] * tensor[3]
        + tensor[0] * tensor[2]
        - tensor[4] * tensor[4]
        + tensor[1] * tensor[2]
        - tensor[5] * tensor[5]
    )
    coherence = 1.0 - 3.0 * minors / (trace * trace + epsilon)
    base = 1.0 + grads[0] * grads[0] + grads[1] * grads[1]
    curvature = (seconds[0] + seconds[1]) / (base * jnp.sqrt(base))
    return coherence, curvature


def on_device(survey, conduct, widths):
    h = HALO
    batch = lax.axis_index("segment")
    field = lax.dynamic_index_in_dim(survey, batch, 0, keepdims=False)
    coeffs = lax.dynamic_index_in_dim(conduct, batch, 1, keepdims=False).astype(jnp.float32)
    width = lax.dynamic_index_in_dim(widths[:, 0], batch, 0, keepdims=False)
    rows, cols, samples = field.shape
    live = (jnp.arange(rows, dtype=jnp.int32) < width)[:, None, None]

    wide = diffusion_columns(jnp.concatenate([field[None], coeffs], 0))
    grown = diffusion_rows(wide, width, cols)
    masks = face_masks(width, rows, cols, samples, h, cols)
    values, coeffs_grown = grown[0], grown[1:]
    n_rows = values.shape[0]
    at = 0
    for repeat in range(STEPS):
        lo, hi = repeat + 1, n_rows - repeat - 1
        values = relax_rows(values, coeffs_grown[:, lo - 1 :], masks, lo, hi, at)
        at = lo
    smooth = values[h - at : h - at + rows, cols - h : 2 * cols + h]

    grown = with_rows(smooth, width, h)
    masks = face_masks(width, rows, cols, samples, h, h)
    results = attributes(grown, masks)
    return tuple(jnp.where(live, value[h : h + rows, h : h + cols], 0.0)[None] for value in results)


def solution(mesh):
    placed = (
        P(None, "inline", "xline", None),
        P(None, None, "inline", "xline", None),
        P(None, "inline"),
    )
    return jax.shard_map(
        on_device,
        mesh=mesh,
        in_specs=placed,
        out_specs=(P("segment", "inline", "xline", None), P("segment", "inline", "xline", None)),
        check_vma=False,
    )
```

```python
import jax
import jax.numpy as jnp
from jax import lax
from jax.sharding import PartitionSpec as P

STEPS = 2
HALO = 2


step_size = 0.15
epsilon = 1e-06


def shifted(source, which_axis, offset):
    length = source.shape[which_axis]
    margins = [(0, 0)] * source.ndim
    if offset > 0:
        margins[which_axis] = (0, offset)
        padded = jnp.pad(source, margins)
        return lax.slice_in_dim(padded, offset, offset + length, axis=which_axis)
    margins[which_axis] = (-offset, 0)
    padded = jnp.pad(source, margins)
    return lax.slice_in_dim(padded, 0, length, axis=which_axis)


def neighbor(source, which_axis, offset, opened):
    return jnp.where(opened, shifted(source, which_axis, offset), source)


def moved(value, d_inline, d_xline):
    n_i = lax.axis_size("inline")
    n_x = lax.axis_size("xline")
    if d_xline == 0:
        pairs = [(i, i + d_inline) for i in range(n_i) if 0 <= i + d_inline < n_i]
        return lax.ppermute(value, "inline", pairs)
    if d_inline == 0:
        pairs = [(x, x + d_xline) for x in range(n_x) if 0 <= x + d_xline < n_x]
        return lax.ppermute(value, "xline", pairs)
    pairs = []
    for i in range(n_i):
        for x in range(n_x):
            ti, tx = i + d_inline, x + d_xline
            if 0 <= ti < n_i and 0 <= tx < n_x:
                pairs.append((i * n_x + x, ti * n_x + tx))
    return lax.ppermute(value, ("inline", "xline"), pairs)


def exchanged(to_next, to_prev, axis):
    count = lax.axis_size(axis)
    odd = lax.axis_index(axis) % 2 == 1
    first = [(i, j) for a in range(1, count - 1, 2) for i, j in ((a, a + 1), (a + 1, a))]
    second = [(i, i ^ 1) for i in range(count) if i ^ 1 < count]
    send_first = jnp.where(odd, to_next, to_prev)
    send_second = jnp.where(odd, to_prev, to_next)
    send_second = send_second + 0.0 * send_first[(0,) * send_first.ndim]
    got_first = lax.ppermute(send_first, axis, first)
    got_second = lax.ppermute(send_second, axis, second)
    return jnp.where(odd, got_second, got_first), jnp.where(odd, got_first, got_second)


def with_columns(block, depth):
    ca = block.ndim - 2
    cols = block.shape[ca]
    from_left = moved(lax.slice_in_dim(block, cols - depth, cols, axis=ca), 0, 1)
    from_right = moved(lax.slice_in_dim(block, 0, depth, axis=ca), 0, -1)
    return jnp.concatenate([from_left, block, from_right], ca)


def with_rows(block, width, depth):
    ra = block.ndim - 3
    from_prev, from_next = exchanged(
        lax.dynamic_slice_in_dim(block, width - depth, depth, ra), lax.slice_in_dim(block, 0, depth, axis=ra), "inline"
    )
    return placed_rows(block, from_prev, from_next, width, depth)


def placed_rows(block, from_prev, from_next, width, depth):
    ra = block.ndim - 3
    stacked = jnp.concatenate([from_prev, block, jnp.zeros_like(from_next)], ra)
    return lax.dynamic_update_slice_in_dim(stacked, from_next, depth + width, ra)


def packed(pieces):
    samples = pieces[0].shape[-1]
    return jnp.concatenate([piece.reshape(-1, samples) for piece in pieces], 0)


def unpacked(flat, shapes):
    out, at = [], 0
    for shape in shapes:
        count = 1
        for size in shape[:-1]:
            count *= size
        out.append(flat[at : at + count].reshape(shape))
        at += count
    return out


def diffusion_columns(fields):
    n_f, rows, cols, samples = fields.shape
    far = jnp.stack([fields[0], fields[2]], 0)
    to_right = packed([fields[:, :, 1:], far[:, :, 0]])
    to_left = packed([fields[:, :, : cols - 1], far[:, :, cols - 1]])
    from_left = unpacked(moved(to_right, 0, 1), [(n_f, rows, cols - 1, samples), (2, rows, samples)])
    from_right = unpacked(moved(to_left, 0, -1), [(n_f, rows, cols - 1, samples), (2, rows, samples)])

    def edge(near, outer, outer_first):
        zero = jnp.zeros_like(outer[0])
        column = jnp.stack([outer[0], zero, outer[1], zero], 0)[:, :, None]
        parts = [column, near] if outer_first else [near, column]
        return jnp.concatenate(parts, 2)

    left = edge(from_left[0], from_left[1], True)
    right = edge(from_right[0], from_right[1], False)
    return jnp.concatenate([left, fields, right], 2)


def diffusion_rows(wide, width, cols):
    n_f, rows, n_c, samples = wide.shape
    h = HALO
    near = slice(cols - 3, 2 * cols + 3)
    mid = slice(cols - 2, 2 * cols + 2)

    def pieces(row_near, row_far):
        return packed([row_near[0:3, near], row_near[3, mid], row_far[0:2, mid]])

    last = lax.dynamic_slice_in_dim(wide, width - h, h, 1)
    to_next = pieces(last[:, 1], last[:, 0])
    to_prev = pieces(wide[:, 0], wide[:, 1])
    shapes = [(3, cols + 6, samples), (cols + 4, samples), (2, cols + 4, samples)]

    def rebuilt(flat):
        p_near, p_time, p_far = unpacked(flat, shapes)
        pad_near = [(0, 0), (cols - 3, cols - 3), (0, 0)]
        pad_mid = [(0, 0), (cols - 2, cols - 2), (0, 0)]
        row_near = jnp.concatenate([jnp.pad(p_near, pad_near), jnp.pad(p_time[None], pad_mid)], 0)
        row_far = jnp.pad(jnp.pad(p_far, pad_mid), [(0, 2), (0, 0), (0, 0)])
        return row_near, row_far

    got_prev, got_next = exchanged(to_next, to_prev, "inline")
    prev_near, prev_far = rebuilt(got_prev)
    next_near, next_far = rebuilt(got_next)
    from_prev = jnp.stack([prev_far, prev_near], 1)
    from_next = jnp.stack([next_near, next_far], 1)
    return placed_rows(wide, from_prev, from_next, width, h)


def face_masks(width, rows, cols, samples, row_halo, col_halo):
    inline_pos = lax.axis_index("inline")
    inline_count = lax.axis_size("inline")
    xline_pos = lax.axis_index("xline")
    xline_count = lax.axis_size("xline")
    own_row = jnp.arange(rows + 2 * row_halo, dtype=jnp.int32) - row_halo
    row_up = jnp.logical_not((inline_pos == inline_count - 1) & (own_row == width - 1))
    row_down = jnp.logical_not((inline_pos == 0) & (own_row == 0))
    own_col = jnp.arange(cols + 2 * col_halo, dtype=jnp.int32) - col_halo
    col_up = jnp.logical_not((xline_pos == xline_count - 1) & (own_col == cols - 1))
    col_down = jnp.logical_not((xline_pos == 0) & (own_col == 0))
    sample = jnp.arange(samples, dtype=jnp.int32)
    return [
        (row_up[:, None, None], row_down[:, None, None]),
        (col_up[None, :, None], col_down[None, :, None]),
        ((sample < samples - 1)[None, None, :], (sample > 0)[None, None, :]),
    ]


def near(source, lo, hi, at, which_axis, offset, opened):
    centre = source[lo - at : hi - at]
    if which_axis == 0:
        return jnp.where(opened, source[lo - at + offset : hi - at + offset], centre)
    return jnp.where(opened, shifted(centre, which_axis, offset), centre)


def rows_of(masks, lo, hi):
    rows = masks[0]
    return [(rows[0][lo:hi], rows[1][lo:hi])] + list(masks[1:])


def relax_rows(values, coeffs, masks, lo, hi, at):
    opened = rows_of(masks, lo, hi)
    centre = values[lo - at : hi - at]
    change = jnp.zeros_like(centre)
    for which_axis in range(3):
        kk = coeffs[which_axis]
        k_centre = kk[lo - at : hi - at]
        up_open, down_open = opened[which_axis]
        for offset, mask in ((1, up_open), (-1, down_open)):
            change = change + 0.5 * (k_centre + near(kk, lo, hi, at, which_axis, offset, mask)) * (
                near(values, lo, hi, at, which_axis, offset, mask) - centre
            )
    return centre + step_size * change


def attributes(grown, masks):
    grads = []
    for which_axis in range(3):
        up_open, down_open = masks[which_axis]
        grads.append(
            0.5
            * (neighbor(grown, which_axis, 1, up_open) - neighbor(grown, which_axis, -1, down_open))
        )
    seconds = []
    for which_axis in range(2):
        up_open, down_open = masks[which_axis]
        seconds.append(
            neighbor(grown, which_axis, 1, up_open)
            + neighbor(grown, which_axis, -1, down_open)
            - 2.0 * grown
        )
    combos = [(0, 0), (1, 1), (2, 2), (0, 1), (0, 2), (1, 2)]
    tensor = []
    for first_index, second_index in combos:
        member = grads[first_index] * grads[second_index]
        for which_axis in range(3):
            up_open, down_open = masks[which_axis]
            member = 0.25 * (
                neighbor(member, which_axis, 1, up_open)
                + 2.0 * member
                + neighbor(member, which_axis, -1, down_open)
            )
        tensor.append(member)
    trace = tensor[0] + tensor[1] + tensor[2]
    minors = (
        tensor[0] * tensor[1]
        - tensor[3] * tensor[3]
        + tensor[0] * tensor[2]
        - tensor[4] * tensor[4]
        + tensor[1] * tensor[2]
        - tensor[5] * tensor[5]
    )
    coherence = 1.0 - 3.0 * minors / (trace * trace + epsilon)
    curvature = (seconds[0] + seconds[1]) / (1.0 + grads[0] * grads[0] + grads[1] * grads[1]) ** 1.5
    return coherence, curvature


def on_device(survey, conduct, widths):
    h = HALO
    batch = lax.axis_index("segment")
    field = lax.dynamic_index_in_dim(survey, batch, 0, keepdims=False)
    coeffs = lax.dynamic_index_in_dim(conduct, batch, 1, keepdims=False).astype(jnp.float32)
    width = lax.dynamic_index_in_dim(widths[:, 0], batch, 0, keepdims=False)
    rows, cols, samples = field.shape
    live = (jnp.arange(rows, dtype=jnp.int32) < width)[:, None, None]

    wide = diffusion_columns(jnp.concatenate([field[None], coeffs], 0))
    grown = diffusion_rows(wide, width, cols)
    masks = face_masks(width, rows, cols, samples, h, cols)
    values, coeffs_grown = grown[0], grown[1:]
    n_rows = values.shape[0]
    at = 0
    for repeat in range(STEPS):
        lo, hi = repeat + 1, n_rows - repeat - 1
        values = relax_rows(values, coeffs_grown[:, lo - 1 :], masks, lo, hi, at)
        at = lo
    smooth = values[h - at : h - at + rows, cols - h : 2 * cols + h]

    grown = with_rows(smooth, width, h)
    masks = face_masks(width, rows, cols, samples, h, h)
    results = attributes(grown, masks)
    return tuple(jnp.where(live, value[h : h + rows, h : h + cols], 0.0)[None] for value in results)


def solution(mesh):
    placed = (
        P(None, "inline", "xline", None),
        P(None, None, "inline", "xline", None),
        P(None, "inline"),
    )
    return jax.shard_map(
        on_device,
        mesh=mesh,
        in_specs=placed,
        out_specs=(P("segment", "inline", "xline", None), P("segment", "inline", "xline", None)),
        check_vma=False,
    )
```

```python
import jax
import jax.numpy as jnp
from jax import lax
from jax.sharding import PartitionSpec as P

STEPS = 2
HALO = 2


step_size = 0.15
epsilon = 1e-06


def shifted(source, which_axis, offset):
    length = source.shape[which_axis]
    margins = [(0, 0)] * source.ndim
    if offset > 0:
        margins[which_axis] = (0, offset)
        padded = jnp.pad(source, margins)
        return lax.slice_in_dim(padded, offset, offset + length, axis=which_axis)
    margins[which_axis] = (-offset, 0)
    padded = jnp.pad(source, margins)
    return lax.slice_in_dim(padded, 0, length, axis=which_axis)


def neighbor(source, which_axis, offset, opened):
    return jnp.where(opened, shifted(source, which_axis, offset), source)


def moved(value, d_inline, d_xline):
    n_i = lax.axis_size("inline")
    n_x = lax.axis_size("xline")
    if d_xline == 0:
        pairs = [(i, i + d_inline) for i in range(n_i) if 0 <= i + d_inline < n_i]
        return lax.ppermute(value, "inline", pairs)
    if d_inline == 0:
        pairs = [(x, x + d_xline) for x in range(n_x) if 0 <= x + d_xline < n_x]
        return lax.ppermute(value, "xline", pairs)
    pairs = []
    for i in range(n_i):
        for x in range(n_x):
            ti, tx = i + d_inline, x + d_xline
            if 0 <= ti < n_i and 0 <= tx < n_x:
                pairs.append((i * n_x + x, ti * n_x + tx))
    return lax.ppermute(value, ("inline", "xline"), pairs)


def with_columns(block, depth):
    ca = block.ndim - 2
    cols = block.shape[ca]
    from_left = moved(lax.slice_in_dim(block, cols - depth, cols, axis=ca), 0, 1)
    from_right = moved(lax.slice_in_dim(block, 0, depth, axis=ca), 0, -1)
    return jnp.concatenate([from_left, block, from_right], ca)


def with_rows(block, width, depth):
    ra = block.ndim - 3
    from_prev = moved(lax.dynamic_slice_in_dim(block, width - depth, depth, ra), 1, 0)
    from_next = moved(lax.slice_in_dim(block, 0, depth, axis=ra), -1, 0)
    return placed_rows(block, from_prev, from_next, width, depth)


def placed_rows(block, from_prev, from_next, width, depth):
    ra = block.ndim - 3
    stacked = jnp.concatenate([from_prev, block, jnp.zeros_like(from_next)], ra)
    return lax.dynamic_update_slice_in_dim(stacked, from_next, depth + width, ra)


def packed(pieces):
    samples = pieces[0].shape[-1]
    return jnp.concatenate([piece.reshape(-1, samples) for piece in pieces], 0)


def unpacked(flat, shapes):
    out, at = [], 0
    for shape in shapes:
        count = 1
        for size in shape[:-1]:
            count *= size
        out.append(flat[at : at + count].reshape(shape))
        at += count
    return out


def diffusion_columns(fields):
    n_f, rows, cols, samples = fields.shape
    far = jnp.stack([fields[0], fields[2]], 0)
    to_right = packed([fields[:, :, 1:], far[:, :, 0]])
    to_left = packed([fields[:, :, : cols - 1], far[:, :, cols - 1]])
    from_left = unpacked(moved(to_right, 0, 1), [(n_f, rows, cols - 1, samples), (2, rows, samples)])
    from_right = unpacked(moved(to_left, 0, -1), [(n_f, rows, cols - 1, samples), (2, rows, samples)])

    def edge(near, outer, outer_first):
        zero = jnp.zeros_like(outer[0])
        column = jnp.stack([outer[0], zero, outer[1], zero], 0)[:, :, None]
        parts = [column, near] if outer_first else [near, column]
        return jnp.concatenate(parts, 2)

    left = edge(from_left[0], from_left[1], True)
    right = edge(from_right[0], from_right[1], False)
    return left, fields, right


def diffusion_rows(parts, width, cols):
    n_f, rows, _, samples = parts[1].shape
    h = HALO
    near = slice(cols - 3, 2 * cols + 3)
    mid = slice(cols - 2, 2 * cols + 2)

    def pieces(row_near, row_far):
        return packed([row_near[0:3, near], row_near[3, mid], row_far[0:2, mid]])

    def rows_at(start):
        return jnp.concatenate([lax.dynamic_slice_in_dim(part, start, h, 1) for part in parts], 2)

    last = rows_at(width - h)
    first = jnp.concatenate([part[:, :h] for part in parts], 2)
    wide = jnp.concatenate(parts, 2)
    to_next = pieces(last[:, 1], last[:, 0])
    to_prev = pieces(first[:, 0], first[:, 1])
    shapes = [(3, cols + 6, samples), (cols + 4, samples), (2, cols + 4, samples)]

    def rebuilt(flat):
        p_near, p_time, p_far = unpacked(flat, shapes)
        pad_near = [(0, 0), (cols - 3, cols - 3), (0, 0)]
        pad_mid = [(0, 0), (cols - 2, cols - 2), (0, 0)]
        row_near = jnp.concatenate([jnp.pad(p_near, pad_near), jnp.pad(p_time[None], pad_mid)], 0)
        row_far = jnp.pad(jnp.pad(p_far, pad_mid), [(0, 2), (0, 0), (0, 0)])
        return row_near, row_far

    prev_near, prev_far = rebuilt(moved(to_next, 1, 0))
    next_near, next_far = rebuilt(moved(to_prev, -1, 0))
    from_prev = jnp.stack([prev_far, prev_near], 1)
    from_next = jnp.stack([next_near, next_far], 1)
    return placed_rows(wide, from_prev, from_next, width, h)


def face_masks(width, rows, cols, samples, row_halo, col_halo):
    inline_pos = lax.axis_index("inline")
    inline_count = lax.axis_size("inline")
    xline_pos = lax.axis_index("xline")
    xline_count = lax.axis_size("xline")
    own_row = jnp.arange(rows + 2 * row_halo, dtype=jnp.int32) - row_halo
    row_up = jnp.logical_not((inline_pos == inline_count - 1) & (own_row == width - 1))
    row_down = jnp.logical_not((inline_pos == 0) & (own_row == 0))
    own_col = jnp.arange(cols + 2 * col_halo, dtype=jnp.int32) - col_halo
    col_up = jnp.logical_not((xline_pos == xline_count - 1) & (own_col == cols - 1))
    col_down = jnp.logical_not((xline_pos == 0) & (own_col == 0))
    sample = jnp.arange(samples, dtype=jnp.int32)
    return [
        (row_up[:, None, None], row_down[:, None, None]),
        (col_up[None, :, None], col_down[None, :, None]),
        ((sample < samples - 1)[None, None, :], (sample > 0)[None, None, :]),
    ]


def near(source, lo, hi, at, which_axis, offset, opened):
    centre = source[lo - at : hi - at]
    if which_axis == 0:
        return jnp.where(opened, source[lo - at + offset : hi - at + offset], centre)
    return jnp.where(opened, shifted(centre, which_axis, offset), centre)


def rows_of(masks, lo, hi):
    rows = masks[0]
    return [(rows[0][lo:hi], rows[1][lo:hi])] + list(masks[1:])


def relax_rows(values, coeffs, masks, lo, hi, at):
    opened = rows_of(masks, lo, hi)
    centre = values[lo - at : hi - at]
    change = jnp.zeros_like(centre)
    for which_axis in range(3):
        kk = coeffs[which_axis]
        k_centre = kk[lo - at : hi - at]
        up_open, down_open = opened[which_axis]
        for offset, mask in ((1, up_open), (-1, down_open)):
            change = change + 0.5 * (k_centre + near(kk, lo, hi, at, which_axis, offset, mask)) * (
                near(values, lo, hi, at, which_axis, offset, mask) - centre
            )
    return centre + step_size * change


def attributes(grown, masks):
    grads = []
    for which_axis in range(3):
        up_open, down_open = masks[which_axis]
        grads.append(
            0.5
            * (neighbor(grown, which_axis, 1, up_open) - neighbor(grown, which_axis, -1, down_open))
        )
    seconds = []
    for which_axis in range(2):
        up_open, down_open = masks[which_axis]
        seconds.append(
            neighbor(grown, which_axis, 1, up_open)
            + neighbor(grown, which_axis, -1, down_open)
            - 2.0 * grown
        )
    combos = [(0, 0), (1, 1), (2, 2), (0, 1), (0, 2), (1, 2)]
    tensor = []
    for first_index, second_index in combos:
        member = grads[first_index] * grads[second_index]
        for which_axis in range(3):
            up_open, down_open = masks[which_axis]
            member = 0.25 * (
                neighbor(member, which_axis, 1, up_open)
                + 2.0 * member
                + neighbor(member, which_axis, -1, down_open)
            )
        tensor.append(member)
    trace = tensor[0] + tensor[1] + tensor[2]
    minors = (
        tensor[0] * tensor[1]
        - tensor[3] * tensor[3]
        + tensor[0] * tensor[2]
        - tensor[4] * tensor[4]
        + tensor[1] * tensor[2]
        - tensor[5] * tensor[5]
    )
    coherence = 1.0 - 3.0 * minors / (trace * trace + epsilon)
    curvature = (seconds[0] + seconds[1]) / (1.0 + grads[0] * grads[0] + grads[1] * grads[1]) ** 1.5
    return coherence, curvature


def on_device(survey, conduct, widths):
    h = HALO
    batch = lax.axis_index("segment")
    field = lax.dynamic_index_in_dim(survey, batch, 0, keepdims=False)
    coeffs = lax.dynamic_index_in_dim(conduct, batch, 1, keepdims=False).astype(jnp.float32)
    width = lax.dynamic_index_in_dim(widths[:, 0], batch, 0, keepdims=False)
    rows, cols, samples = field.shape
    live = (jnp.arange(rows, dtype=jnp.int32) < width)[:, None, None]

    wide = diffusion_columns(jnp.concatenate([field[None], coeffs], 0))
    grown = diffusion_rows(wide, width, cols)
    masks = face_masks(width, rows, cols, samples, h, cols)
    values, coeffs_grown = grown[0], grown[1:]
    n_rows = values.shape[0]
    at = 0
    for repeat in range(STEPS):
        lo, hi = repeat + 1, n_rows - repeat - 1
        values = relax_rows(values, coeffs_grown[:, lo - 1 :], masks, lo, hi, at)
        at = lo
    smooth = values[h - at : h - at + rows, cols - h : 2 * cols + h]

    grown = with_rows(smooth, width, h)
    masks = face_masks(width, rows, cols, samples, h, h)
    results = attributes(grown, masks)
    return tuple(jnp.where(live, value[h : h + rows, h : h + cols], 0.0)[None] for value in results)


def solution(mesh):
    placed = (
        P(None, "inline", "xline", None),
        P(None, None, "inline", "xline", None),
        P(None, "inline"),
    )
    return jax.shard_map(
        on_device,
        mesh=mesh,
        in_specs=placed,
        out_specs=(P("segment", "inline", "xline", None), P("segment", "inline", "xline", None)),
        check_vma=False,
    )
```

```python
import jax
import jax.numpy as jnp
from jax import lax
from jax.sharding import PartitionSpec as P

STEPS = 2
HALO = 2


step_size = 0.15
epsilon = 1e-06


def shifted(source, which_axis, offset):
    length = source.shape[which_axis]
    margins = [(0, 0)] * source.ndim
    if offset > 0:
        margins[which_axis] = (0, offset)
        padded = jnp.pad(source, margins)
        return lax.slice_in_dim(padded, offset, offset + length, axis=which_axis)
    margins[which_axis] = (-offset, 0)
    padded = jnp.pad(source, margins)
    return lax.slice_in_dim(padded, 0, length, axis=which_axis)


def neighbor(source, which_axis, offset, opened):
    return jnp.where(opened, shifted(source, which_axis, offset), source)


def moved(value, d_inline, d_xline):
    n_i = lax.axis_size("inline")
    n_x = lax.axis_size("xline")
    if d_xline == 0:
        pairs = [(i, i + d_inline) for i in range(n_i) if 0 <= i + d_inline < n_i]
        return lax.ppermute(value, "inline", pairs)
    if d_inline == 0:
        pairs = [(x, x + d_xline) for x in range(n_x) if 0 <= x + d_xline < n_x]
        return lax.ppermute(value, "xline", pairs)
    pairs = []
    for i in range(n_i):
        for x in range(n_x):
            ti, tx = i + d_inline, x + d_xline
            if 0 <= ti < n_i and 0 <= tx < n_x:
                pairs.append((i * n_x + x, ti * n_x + tx))
    return lax.ppermute(value, ("inline", "xline"), pairs)


def with_columns(block, depth):
    ca = block.ndim - 2
    cols = block.shape[ca]
    from_left = moved(lax.slice_in_dim(block, cols - depth, cols, axis=ca), 0, 1)
    from_right = moved(lax.slice_in_dim(block, 0, depth, axis=ca), 0, -1)
    return jnp.concatenate([from_left, block, from_right], ca)


def with_rows(block, width, depth):
    ra = block.ndim - 3
    from_prev = moved(lax.dynamic_slice_in_dim(block, width - depth, depth, ra), 1, 0)
    from_next = moved(lax.slice_in_dim(block, 0, depth, axis=ra), -1, 0)
    return placed_rows(block, from_prev, from_next, width, depth)


def placed_rows(block, from_prev, from_next, width, depth):
    ra = block.ndim - 3
    stacked = jnp.concatenate([from_prev, block, jnp.zeros_like(from_next)], ra)
    return lax.dynamic_update_slice_in_dim(stacked, from_next, depth + width, ra)


def packed(pieces):
    samples = pieces[0].shape[-1]
    return jnp.concatenate([piece.reshape(-1, samples) for piece in pieces], 0)


def unpacked(flat, shapes):
    out, at = [], 0
    for shape in shapes:
        count = 1
        for size in shape[:-1]:
            count *= size
        out.append(flat[at : at + count].reshape(shape))
        at += count
    return out


def diffusion_columns(fields):
    n_f, rows, cols, samples = fields.shape
    far = jnp.stack([fields[0], fields[2]], 0)
    to_right = packed([fields[:, :, 1:], far[:, :, 0]])
    to_left = packed([fields[:, :, : cols - 1], far[:, :, cols - 1]])
    from_left = unpacked(moved(to_right, 0, 1), [(n_f, rows, cols - 1, samples), (2, rows, samples)])
    from_right = unpacked(moved(to_left, 0, -1), [(n_f, rows, cols - 1, samples), (2, rows, samples)])

    def edge(near, outer, outer_first):
        zero = jnp.zeros_like(outer[0])
        column = jnp.stack([outer[0], zero, outer[1], zero], 0)[:, :, None]
        parts = [column, near] if outer_first else [near, column]
        return jnp.concatenate(parts, 2)

    left = edge(from_left[0], from_left[1], True)
    right = edge(from_right[0], from_right[1], False)
    return left, fields, right


def diffusion_rows(parts, width, cols):
    n_f, rows, _, samples = parts[1].shape
    h = HALO
    near = slice(cols - 3, 2 * cols + 3)
    mid = slice(cols - 2, 2 * cols + 2)

    def pieces(row_near, row_far):
        return packed([row_near[0:3, near], row_near[3, mid], row_far[0:2, mid]])

    def rows_at(start):
        return jnp.concatenate([lax.dynamic_slice_in_dim(part, start, h, 1) for part in parts], 2)

    last = rows_at(width - h)
    first = jnp.concatenate([part[:, :h] for part in parts], 2)
    wide = jnp.concatenate(parts, 2)
    to_next = pieces(last[:, 1], last[:, 0])
    to_prev = pieces(first[:, 0], first[:, 1])
    shapes = [(3, cols + 6, samples), (cols + 4, samples), (2, cols + 4, samples)]

    def rebuilt(flat):
        p_near, p_time, p_far = unpacked(flat, shapes)
        pad_near = [(0, 0), (cols - 3, cols - 3), (0, 0)]
        pad_mid = [(0, 0), (cols - 2, cols - 2), (0, 0)]
        row_near = jnp.concatenate([jnp.pad(p_near, pad_near), jnp.pad(p_time[None], pad_mid)], 0)
        row_far = jnp.pad(jnp.pad(p_far, pad_mid), [(0, 2), (0, 0), (0, 0)])
        return row_near, row_far

    prev_near, prev_far = rebuilt(moved(to_next, 1, 0))
    next_near, next_far = rebuilt(moved(to_prev, -1, 0))
    from_prev = jnp.stack([prev_far, prev_near], 1)
    from_next = jnp.stack([next_near, next_far], 1)
    return placed_rows(wide, from_prev, from_next, width, h)


def face_masks(width, rows, cols, samples, row_halo, col_halo):
    inline_pos = lax.axis_index("inline")
    inline_count = lax.axis_size("inline")
    xline_pos = lax.axis_index("xline")
    xline_count = lax.axis_size("xline")
    own_row = jnp.arange(rows + 2 * row_halo, dtype=jnp.int32) - row_halo
    row_up = jnp.logical_not((inline_pos == inline_count - 1) & (own_row == width - 1))
    row_down = jnp.logical_not((inline_pos == 0) & (own_row == 0))
    own_col = jnp.arange(cols + 2 * col_halo, dtype=jnp.int32) - col_halo
    col_up = jnp.logical_not((xline_pos == xline_count - 1) & (own_col == cols - 1))
    col_down = jnp.logical_not((xline_pos == 0) & (own_col == 0))
    sample = jnp.arange(samples, dtype=jnp.int32)
    return [
        (row_up[:, None, None], row_down[:, None, None]),
        (col_up[None, :, None], col_down[None, :, None]),
        ((sample < samples - 1)[None, None, :], (sample > 0)[None, None, :]),
    ]


def near(source, lo, hi, at, which_axis, offset, opened, cols=None):
    cut = slice(None) if cols is None else slice(*cols)
    centre = source[lo - at : hi - at, cut]
    if which_axis == 0:
        return jnp.where(opened, source[lo - at + offset : hi - at + offset, cut], centre)
    if which_axis == 1 and cols is not None:
        return jnp.where(opened, source[lo - at : hi - at, cols[0] + offset : cols[1] + offset], centre)
    return jnp.where(opened, shifted(centre, which_axis, offset), centre)


def rows_of(masks, lo, hi, cols=None):
    rows = masks[0]
    column = masks[1] if cols is None else tuple(m[:, cols[0] : cols[1]] for m in masks[1])
    return [(rows[0][lo:hi], rows[1][lo:hi]), column, masks[2]]


def relax_rows(values, coeffs, masks, lo, hi, at, cols=None):
    opened = rows_of(masks, lo, hi, cols)
    cut = slice(None) if cols is None else slice(*cols)
    centre = values[lo - at : hi - at, cut]
    change = jnp.zeros_like(centre)
    for which_axis in range(3):
        kk = coeffs[which_axis]
        k_centre = kk[lo - at : hi - at, cut]
        up_open, down_open = opened[which_axis]
        for offset, mask in ((1, up_open), (-1, down_open)):
            change = change + 0.5 * (k_centre + near(kk, lo, hi, at, which_axis, offset, mask, cols)) * (
                near(values, lo, hi, at, which_axis, offset, mask, cols) - centre
            )
    return centre + step_size * change


def attributes(grown, masks):
    grads = []
    for which_axis in range(3):
        up_open, down_open = masks[which_axis]
        grads.append(
            0.5
            * (neighbor(grown, which_axis, 1, up_open) - neighbor(grown, which_axis, -1, down_open))
        )
    seconds = []
    for which_axis in range(2):
        up_open, down_open = masks[which_axis]
        seconds.append(
            neighbor(grown, which_axis, 1, up_open)
            + neighbor(grown, which_axis, -1, down_open)
            - 2.0 * grown
        )
    combos = [(0, 0), (1, 1), (2, 2), (0, 1), (0, 2), (1, 2)]
    tensor = []
    for first_index, second_index in combos:
        member = grads[first_index] * grads[second_index]
        for which_axis in range(3):
            up_open, down_open = masks[which_axis]
            member = 0.25 * (
                neighbor(member, which_axis, 1, up_open)
                + 2.0 * member
                + neighbor(member, which_axis, -1, down_open)
            )
        tensor.append(member)
    trace = tensor[0] + tensor[1] + tensor[2]
    minors = (
        tensor[0] * tensor[1]
        - tensor[3] * tensor[3]
        + tensor[0] * tensor[2]
        - tensor[4] * tensor[4]
        + tensor[1] * tensor[2]
        - tensor[5] * tensor[5]
    )
    coherence = 1.0 - 3.0 * minors / (trace * trace + epsilon)
    curvature = (seconds[0] + seconds[1]) / (1.0 + grads[0] * grads[0] + grads[1] * grads[1]) ** 1.5
    return coherence, curvature


def on_device(survey, conduct, widths):
    h = HALO
    batch = lax.axis_index("segment")
    field = lax.dynamic_index_in_dim(survey, batch, 0, keepdims=False)
    coeffs = lax.dynamic_index_in_dim(conduct, batch, 1, keepdims=False).astype(jnp.float32)
    width = lax.dynamic_index_in_dim(widths[:, 0], batch, 0, keepdims=False)
    rows, cols, samples = field.shape
    live = (jnp.arange(rows, dtype=jnp.int32) < width)[:, None, None]

    wide = diffusion_columns(jnp.concatenate([field[None], coeffs], 0))
    grown = diffusion_rows(wide, width, cols)
    masks = face_masks(width, rows, cols, samples, h, cols)
    values, coeffs_grown = grown[0], grown[1:]
    n_rows = values.shape[0]
    at = 0
    for repeat in range(STEPS):
        lo, hi = repeat + 1, n_rows - repeat - 1
        kept = (cols - h, 2 * cols + h) if repeat == STEPS - 1 else None
        values = relax_rows(values, coeffs_grown[:, lo - 1 :], masks, lo, hi, at, kept)
        at = lo
    smooth = values[h - at : h - at + rows]

    grown = with_rows(smooth, width, h)
    masks = face_masks(width, rows, cols, samples, h, h)
    results = attributes(grown, masks)
    return tuple(jnp.where(live, value[h : h + rows, h : h + cols], 0.0)[None] for value in results)


def solution(mesh):
    placed = (
        P(None, "inline", "xline", None),
        P(None, None, "inline", "xline", None),
        P(None, "inline"),
    )
    return jax.shard_map(
        on_device,
        mesh=mesh,
        in_specs=placed,
        out_specs=(P("segment", "inline", "xline", None), P("segment", "inline", "xline", None)),
        check_vma=False,
    )
```

```python
import jax
import jax.numpy as jnp
from jax import lax
from jax.sharding import PartitionSpec as P

STEPS = 2
HALO = 2


step_size = 0.15
epsilon = 1e-06


def shifted(source, which_axis, offset):
    length = source.shape[which_axis]
    margins = [(0, 0)] * source.ndim
    if offset > 0:
        margins[which_axis] = (0, offset)
        padded = jnp.pad(source, margins)
        return lax.slice_in_dim(padded, offset, offset + length, axis=which_axis)
    margins[which_axis] = (-offset, 0)
    padded = jnp.pad(source, margins)
    return lax.slice_in_dim(padded, 0, length, axis=which_axis)


def neighbor(source, which_axis, offset, opened):
    return jnp.where(opened, shifted(source, which_axis, offset), source)


def moved(value, d_inline, d_xline):
    n_i = lax.axis_size("inline")
    n_x = lax.axis_size("xline")
    if d_xline == 0:
        pairs = [(i, i + d_inline) for i in range(n_i) if 0 <= i + d_inline < n_i]
        return lax.ppermute(value, "inline", pairs)
    if d_inline == 0:
        pairs = [(x, x + d_xline) for x in range(n_x) if 0 <= x + d_xline < n_x]
        return lax.ppermute(value, "xline", pairs)
    pairs = []
    for i in range(n_i):
        for x in range(n_x):
            ti, tx = i + d_inline, x + d_xline
            if 0 <= ti < n_i and 0 <= tx < n_x:
                pairs.append((i * n_x + x, ti * n_x + tx))
    return lax.ppermute(value, ("inline", "xline"), pairs)


def with_columns(block, depth):
    ca = block.ndim - 2
    cols = block.shape[ca]
    from_left = moved(lax.slice_in_dim(block, cols - depth, cols, axis=ca), 0, 1)
    from_right = moved(lax.slice_in_dim(block, 0, depth, axis=ca), 0, -1)
    return jnp.concatenate([from_left, block, from_right], ca)


def with_rows(block, width, depth):
    cols = block.shape[1]
    last = lax.dynamic_slice_in_dim(block, width - depth, depth, 0)
    to_next = jnp.concatenate([last[1], last[0, 1 : cols - 1]], 0)
    to_prev = jnp.concatenate([block[0], block[1, 1 : cols - 1]], 0)

    def rebuilt(flat):
        return flat[:cols], jnp.pad(flat[cols:], [(1, 1), (0, 0)])

    prev_near, prev_far = rebuilt(moved(to_next, 1, 0))
    next_near, next_far = rebuilt(moved(to_prev, -1, 0))
    from_prev = jnp.stack([prev_far, prev_near], 0)
    from_next = jnp.stack([next_near, next_far], 0)
    return placed_rows(block, from_prev, from_next, width, depth)


def placed_rows(block, from_prev, from_next, width, depth):
    ra = block.ndim - 3
    stacked = jnp.concatenate([from_prev, block, jnp.zeros_like(from_next)], ra)
    return lax.dynamic_update_slice_in_dim(stacked, from_next, depth + width, ra)


def packed(pieces):
    samples = pieces[0].shape[-1]
    return jnp.concatenate([piece.reshape(-1, samples) for piece in pieces], 0)


def unpacked(flat, shapes):
    out, at = [], 0
    for shape in shapes:
        count = 1
        for size in shape[:-1]:
            count *= size
        out.append(flat[at : at + count].reshape(shape))
        at += count
    return out


def diffusion_columns(fields):
    n_f, rows, cols, samples = fields.shape
    far = jnp.stack([fields[0], fields[2]], 0)
    to_right = packed([fields[:, :, 1:], far[:, :, 0]])
    to_left = packed([fields[:, :, : cols - 1], far[:, :, cols - 1]])
    from_left = unpacked(moved(to_right, 0, 1), [(n_f, rows, cols - 1, samples), (2, rows, samples)])
    from_right = unpacked(moved(to_left, 0, -1), [(n_f, rows, cols - 1, samples), (2, rows, samples)])

    def edge(near, outer, outer_first):
        zero = jnp.zeros_like(outer[0])
        column = jnp.stack([outer[0], zero, outer[1], zero], 0)[:, :, None]
        parts = [column, near] if outer_first else [near, column]
        return jnp.concatenate(parts, 2)

    left = edge(from_left[0], from_left[1], True)
    right = edge(from_right[0], from_right[1], False)
    return left, fields, right


def diffusion_rows(parts, width, cols):
    n_f, rows, _, samples = parts[1].shape
    h = HALO
    near = slice(cols - 3, 2 * cols + 3)
    mid = slice(cols - 2, 2 * cols + 2)

    def pieces(row_near, row_far):
        return packed([row_near[0:3, near], row_near[3, mid], row_far[0:2, mid]])

    def rows_at(start):
        return jnp.concatenate([lax.dynamic_slice_in_dim(part, start, h, 1) for part in parts], 2)

    last = rows_at(width - h)
    first = jnp.concatenate([part[:, :h] for part in parts], 2)
    wide = jnp.concatenate(parts, 2)
    to_next = pieces(last[:, 1], last[:, 0])
    to_prev = pieces(first[:, 0], first[:, 1])
    shapes = [(3, cols + 6, samples), (cols + 4, samples), (2, cols + 4, samples)]

    def rebuilt(flat):
        p_near, p_time, p_far = unpacked(flat, shapes)
        pad_near = [(0, 0), (cols - 3, cols - 3), (0, 0)]
        pad_mid = [(0, 0), (cols - 2, cols - 2), (0, 0)]
        row_near = jnp.concatenate([jnp.pad(p_near, pad_near), jnp.pad(p_time[None], pad_mid)], 0)
        row_far = jnp.pad(jnp.pad(p_far, pad_mid), [(0, 2), (0, 0), (0, 0)])
        return row_near, row_far

    prev_near, prev_far = rebuilt(moved(to_next, 1, 0))
    next_near, next_far = rebuilt(moved(to_prev, -1, 0))
    from_prev = jnp.stack([prev_far, prev_near], 1)
    from_next = jnp.stack([next_near, next_far], 1)
    return placed_rows(wide, from_prev, from_next, width, h)


def face_masks(width, rows, cols, samples, row_halo, col_halo):
    inline_pos = lax.axis_index("inline")
    inline_count = lax.axis_size("inline")
    xline_pos = lax.axis_index("xline")
    xline_count = lax.axis_size("xline")
    own_row = jnp.arange(rows + 2 * row_halo, dtype=jnp.int32) - row_halo
    row_up = jnp.logical_not((inline_pos == inline_count - 1) & (own_row == width - 1))
    row_down = jnp.logical_not((inline_pos == 0) & (own_row == 0))
    own_col = jnp.arange(cols + 2 * col_halo, dtype=jnp.int32) - col_halo
    col_up = jnp.logical_not((xline_pos == xline_count - 1) & (own_col == cols - 1))
    col_down = jnp.logical_not((xline_pos == 0) & (own_col == 0))
    sample = jnp.arange(samples, dtype=jnp.int32)
    return [
        (row_up[:, None, None], row_down[:, None, None]),
        (col_up[None, :, None], col_down[None, :, None]),
        ((sample < samples - 1)[None, None, :], (sample > 0)[None, None, :]),
    ]


def near(source, lo, hi, at, which_axis, offset, opened, cols=None):
    cut = slice(None) if cols is None else slice(*cols)
    centre = source[lo - at : hi - at, cut]
    if which_axis == 0:
        return jnp.where(opened, source[lo - at + offset : hi - at + offset, cut], centre)
    if which_axis == 1 and cols is not None:
        return jnp.where(opened, source[lo - at : hi - at, cols[0] + offset : cols[1] + offset], centre)
    return jnp.where(opened, shifted(centre, which_axis, offset), centre)


def rows_of(masks, lo, hi, cols=None):
    rows = masks[0]
    column = masks[1] if cols is None else tuple(m[:, cols[0] : cols[1]] for m in masks[1])
    return [(rows[0][lo:hi], rows[1][lo:hi]), column, masks[2]]


def relax_rows(values, coeffs, masks, lo, hi, at, cols=None):
    opened = rows_of(masks, lo, hi, cols)
    cut = slice(None) if cols is None else slice(*cols)
    centre = values[lo - at : hi - at, cut]
    change = jnp.zeros_like(centre)
    for which_axis in range(3):
        kk = coeffs[which_axis]
        k_centre = kk[lo - at : hi - at, cut]
        up_open, down_open = opened[which_axis]
        for offset, mask in ((1, up_open), (-1, down_open)):
            change = change + 0.5 * (k_centre + near(kk, lo, hi, at, which_axis, offset, mask, cols)) * (
                near(values, lo, hi, at, which_axis, offset, mask, cols) - centre
            )
    return centre + step_size * change


def attributes(grown, masks):
    grads = []
    for which_axis in range(3):
        up_open, down_open = masks[which_axis]
        grads.append(
            0.5
            * (neighbor(grown, which_axis, 1, up_open) - neighbor(grown, which_axis, -1, down_open))
        )
    seconds = []
    for which_axis in range(2):
        up_open, down_open = masks[which_axis]
        seconds.append(
            neighbor(grown, which_axis, 1, up_open)
            + neighbor(grown, which_axis, -1, down_open)
            - 2.0 * grown
        )
    combos = [(0, 0), (1, 1), (2, 2), (0, 1), (0, 2), (1, 2)]
    tensor = []
    for first_index, second_index in combos:
        member = grads[first_index] * grads[second_index]
        for which_axis in range(3):
            up_open, down_open = masks[which_axis]
            member = 0.25 * (
                neighbor(member, which_axis, 1, up_open)
                + 2.0 * member
                + neighbor(member, which_axis, -1, down_open)
            )
        tensor.append(member)
    trace = tensor[0] + tensor[1] + tensor[2]
    minors = (
        tensor[0] * tensor[1]
        - tensor[3] * tensor[3]
        + tensor[0] * tensor[2]
        - tensor[4] * tensor[4]
        + tensor[1] * tensor[2]
        - tensor[5] * tensor[5]
    )
    coherence = 1.0 - 3.0 * minors / (trace * trace + epsilon)
    curvature = (seconds[0] + seconds[1]) / (1.0 + grads[0] * grads[0] + grads[1] * grads[1]) ** 1.5
    return coherence, curvature


def on_device(survey, conduct, widths):
    h = HALO
    batch = lax.axis_index("segment")
    field = lax.dynamic_index_in_dim(survey, batch, 0, keepdims=False)
    coeffs = lax.dynamic_index_in_dim(conduct, batch, 1, keepdims=False).astype(jnp.float32)
    width = lax.dynamic_index_in_dim(widths[:, 0], batch, 0, keepdims=False)
    rows, cols, samples = field.shape
    live = (jnp.arange(rows, dtype=jnp.int32) < width)[:, None, None]

    wide = diffusion_columns(jnp.concatenate([field[None], coeffs], 0))
    grown = diffusion_rows(wide, width, cols)
    masks = face_masks(width, rows, cols, samples, h, cols)
    values, coeffs_grown = grown[0], grown[1:]
    n_rows = values.shape[0]
    at = 0
    for repeat in range(STEPS):
        lo, hi = repeat + 1, n_rows - repeat - 1
        kept = (cols - h, 2 * cols + h) if repeat == STEPS - 1 else None
        values = relax_rows(values, coeffs_grown[:, lo - 1 :], masks, lo, hi, at, kept)
        at = lo
    smooth = values[h - at : h - at + rows]

    grown = with_rows(smooth, width, h)
    masks = face_masks(width, rows, cols, samples, h, h)
    results = attributes(grown, masks)
    return tuple(jnp.where(live, value[h : h + rows, h : h + cols], 0.0)[None] for value in results)


def solution(mesh):
    placed = (
        P(None, "inline", "xline", None),
        P(None, None, "inline", "xline", None),
        P(None, "inline"),
    )
    return jax.shard_map(
        on_device,
        mesh=mesh,
        in_specs=placed,
        out_specs=(P("segment", "inline", "xline", None), P("segment", "inline", "xline", None)),
        check_vma=False,
    )
```
